256 devices in a mesh: dp: 64 (over x, z, core), rep: 4 (over y).
Axes of the slice: x: 4, y: 4, z: 8, core: 2. Of those that a mesh axis runs over, the one named last changes fastest.
Arguments:
- grad_rows: bfloat16 [48, 1024, 768], P(None, 'dp'), may hold values from -40 to 40
- row_counts: int32 [48, 64], replicated, may hold values from 1 to 16, 768 in all within a row
- owners: int32 [48], replicated, may hold values from 0 to 63, as said below
- momentum: float32 [64, 4, 768, 768], P('dp', 'rep'), may hold values from -1.8 to 1.8
Outputs:
- update_rows: bfloat16 [48, 1024, 768], P(None, 'dp')
- momentum_out: float32 [64, 4, 768, 768], P('dp', 'rep')
The draws below stay inside these ranges and needn't reach their ends.
Inputs may be any that keep to these rules, and one draw needn't show every extreme that they name: `owners`: each dp index owns at most 4 matrices, and some index owns exactly 4. Each row of row_counts sums to 768 and has an entry equal to 16.
All inputs are finite; a program needn't handle non-finite values.
Results may differ from the reference program's by a relative error of at most 0.035.
Values may be sent and summed in bfloat16 or wider, within the bound.
No kernel may reach another device: no remote copies, remote signals or barrier semaphores. Data moves between devices by JAX's collectives and lax.ppermute only.
A program may use at most 64 MiB of HBM per device.

```python
import math
import jax
import jax.numpy as jnp
import numpy as np
from jax import lax

D = 768
NS_ITERS = 5
MATS = 48
CAP = 16
N_DP = 64
N_REP = 4


def draw_grad_rows(key, part):
    values = jax.random.normal(jax.random.fold_in(key, 11), (MATS, N_DP * CAP, D), jnp.float32)
    values = jnp.clip(values, -40.0, 40.0)
    return values.astype(jnp.bfloat16)


def draw_owners(key, part):
    busiest = jax.random.randint(jax.random.fold_in(key, 21), (), 0, N_DP, jnp.int32)
    seat_total = N_REP * (N_DP - 1)
    seat_range = jnp.arange(seat_total, dtype=jnp.int32)
    scores = jax.random.permutation(jax.random.fold_in(key, 22), seat_total).astype(jnp.int32)
    low_seat = jnp.mod(N_DP - 1 - busiest, N_DP - 1).astype(jnp.int32)
    high_seat = jnp.mod(N_DP - 2 - busiest, N_DP - 1).astype(jnp.int32)
    forced = (seat_range == low_seat) | (seat_range == high_seat)
    scores = jnp.where(forced, scores - seat_total, scores).astype(jnp.int32)
    seat_ids = jnp.argsort(scores, stable=True)[:MATS - N_REP].astype(jnp.int32)
    others = ((busiest + 1 + seat_ids % (N_DP - 1)) % N_DP).astype(jnp.int32)
    listed = jnp.concatenate([jnp.zeros((N_REP,), jnp.int32) + busiest, others])
    order_ids = jax.random.permutation(jax.random.fold_in(key, 23), MATS)
    return listed[order_ids].astype(jnp.int32)


def steps_of(stream_key, shape, cuts, smallest, largest):
    level, own = 1.0, jax.random.fold_in(stream_key, 6)
    for dim, parts in cuts:
        draws = jnp.exp(jax.random.uniform(jax.random.fold_in(own, dim), (parts,), jnp.float32, smallest / len(cuts), largest / len(cuts)))
        level = level * jnp.repeat(draws, shape[dim] // parts).reshape([-1 if axis == dim else 1 for axis in range(len(shape))])
    return level


def split_up(count, total, reach, lean):
    portions = [(1 << 20) // math.isqrt(rank ** lean) + 1 for rank in range(2, count + 1)]
    rest, given = total - reach - (count - 1), [1] * (count - 1)
    while rest > 0:
        movable = [i for i in range(count - 1) if given[i] < reach]
        whole, budget = sum([portions[i] for i in movable]), rest
        for i in movable:
            addition = min(reach - given[i], max(1, budget * portions[i] // whole), rest)
            given[i] = given[i] + addition
            rest = rest - addition
    return np.array([reach] + given)


def uneven_parts(stream_key, number_of, total, most, lean):
    if number_of == 2:
        one = jax.random.randint(stream_key, (), max(1, total - most), min(most, total - 1) + 1)
        return jnp.stack([one, total - one])
    tallies = jnp.asarray(split_up(number_of, total, most, lean), jnp.int32)
    twos = (number_of - 1) // 2
    giver, sink = tallies[1:1 + 2 * twos:2], tallies[2:2 + 2 * twos:2]
    room = jnp.minimum(giver - 1, most - sink)
    shifted = jax.random.randint(jax.random.fold_in(stream_key, 1), (twos,), 0, 1 << 20) % (room + 1)
    tallies = tallies.at[1:1 + 2 * twos:2].set(giver - shifted).at[2:2 + 2 * twos:2].set(sink + shifted)
    return tallies[jax.random.permutation(jax.random.fold_in(stream_key, 2), number_of)]


def gaussian(stream_key, shape, deviation, limit, split=(), kind=jnp.bfloat16):
    array = deviation * jax.random.normal(stream_key, shape, jnp.float32)
    if split:
        array = array * steps_of(stream_key, shape, split, -0.22, 0.18)
    return jnp.clip(array, -limit, limit).astype(kind)


def setup_inputs(seed: int = 0) -> dict:
    streams_of = jax.random.split(jax.random.key(seed), 5)
    grad_rows = draw_grad_rows(jax.random.fold_in(streams_of[4], 71), 0)
    row_counts = jax.vmap(lambda own: uneven_parts(own, N_DP, D, CAP, 1))(jax.random.split(streams_of[1], MATS)).reshape((MATS, N_DP)).astype(jnp.int32)
    owners = draw_owners(jax.random.fold_in(streams_of[4], 71), 0)
    momentum = gaussian(streams_of[3], (N_DP, N_REP, D, D), 0.3, 1.8, ((0, 64), (1, 4)), jnp.float32)
    return {"grad_rows": grad_rows, "row_counts": row_counts, "owners": owners, "momentum": momentum}


momentum_decay = 0.95
grad_share = 0.05
epsilon = 1e-06
quintic_one = 3.4445
quintic_two = -4.775
quintic_three = 2.0315

def slots_of(owners):
    total = owners.shape[0]
    same_owner = owners[:, None] == owners[None, :]
    position = jnp.arange(total, dtype=jnp.int32)
    earlier = position[None, :] < position[:, None]
    return lax.optimization_barrier(jnp.sum((same_owner & earlier).astype(jnp.int32), axis=1)).astype(jnp.int32)

def gather_index(counts, capacity, extent):
    starts = (jnp.cumsum(counts) - counts).astype(jnp.int32)
    row_ids = jnp.arange(extent, dtype=jnp.int32)
    holder = (lax.optimization_barrier(jnp.sum((starts[None, :] <= row_ids[:, None]).astype(jnp.int32), axis=1)) - 1).astype(jnp.int32)
    first_row = jnp.take(starts, holder).astype(jnp.int32)
    return (holder * capacity + jnp.clip(row_ids - first_row, 0, capacity - 1)).astype(jnp.int32)

def return_index(counts, capacity, extent):
    starts = (jnp.cumsum(counts) - counts).astype(jnp.int32)
    offsets = jnp.arange(capacity, dtype=jnp.int32)
    positions = (starts[:, None] + offsets[None, :]).astype(jnp.int32)
    usable = offsets[None, :] < counts[:, None]
    return (jnp.clip(positions, 0, extent - 1).astype(jnp.int32), usable)

def orthogonalize(full_grad, moment):
    extent = full_grad.shape[0]
    gradient = full_grad.astype(jnp.float32)
    moment_new = momentum_decay * moment + grad_share * gradient
    blended = grad_share * gradient + momentum_decay * moment_new
    frob_norm = jnp.sqrt(jnp.sum(blended * blended)) + epsilon
    iterate = (blended / frob_norm).astype(jnp.bfloat16)
    result = iterate
    for iteration in range(NS_ITERS):
        gram_matrix = lax.dot_general(iterate, iterate, (((1,), (1,)), ((), ())), preferred_element_type=jnp.float32).astype(jnp.bfloat16)
        square = jnp.dot(gram_matrix, gram_matrix, preferred_element_type=jnp.float32)
        polynomial = (quintic_two * gram_matrix.astype(jnp.float32) + quintic_three * square).astype(jnp.bfloat16)
        next_iter = quintic_one * iterate.astype(jnp.float32) + jnp.dot(polynomial, iterate, preferred_element_type=jnp.float32)
        if iteration + 1 < NS_ITERS:
            iterate = next_iter.astype(jnp.bfloat16)
        else:
            result = (math.sqrt(extent) * next_iter).astype(jnp.bfloat16)
    return (result, moment_new)

def reference(grad_rows, row_counts, owners, momentum):
    matrices = grad_rows.shape[0]
    shards = row_counts.shape[1]
    capacity = grad_rows.shape[1] // shards
    extent = grad_rows.shape[2]
    slot_ids = slots_of(owners)
    row_index = jax.vmap(lambda counts: gather_index(counts, capacity, extent))(row_counts)
    moments = momentum[owners, slot_ids]

    def per_matrix(inputs):
        rows_here, index_here, moment_here = inputs
        full_grad = jnp.take(rows_here, index_here, axis=0)
        return orthogonalize(full_grad, moment_here)
    updates, moment_new = lax.map(per_matrix, (grad_rows, row_index, moments))
    momentum_out = jnp.zeros_like(momentum).at[owners, slot_ids].set(moment_new)
    positions, usable = jax.vmap(lambda counts: return_index(counts, capacity, extent))(row_counts)
    picked = jax.vmap(lambda update_one, spots_one: jnp.take(update_one, spots_one.reshape(-1), axis=0))(updates, positions)
    update_rows = jnp.where(usable.reshape(matrices, -1)[:, :, None], picked, jnp.zeros_like(picked))
    return (update_rows, momentum_out)
```

```python
import math

import jax
import jax.numpy as jnp
from jax import lax
from jax.sharding import PartitionSpec as P

NS_ITERS = 5


momentum_decay = 0.95
grad_share = 0.05
epsilon = 1e-06
quintic_one = 3.4445
quintic_two = -4.775
quintic_three = 2.0315


def slots_of(owners):
    total = owners.shape[0]
    same_owner = owners[:, None] == owners[None, :]
    position = jnp.arange(total, dtype=jnp.int32)
    earlier = position[None, :] < position[:, None]
    return jnp.sum((same_owner & earlier).astype(jnp.int32), axis=1)


def exclusive_starts(counts):
    shards = counts.shape[0]
    ids = jnp.arange(shards, dtype=jnp.int32)
    before = ids[None, :] < ids[:, None]
    return jnp.sum(jnp.where(before, counts[None, :], 0), axis=1)


def orthogonalize(full_grad, moment):
    extent = full_grad.shape[0]
    gradient = full_grad.astype(jnp.float32)
    moment_new = momentum_decay * moment + grad_share * gradient
    blended = grad_share * gradient + momentum_decay * moment_new
    frob_norm = jnp.sqrt(jnp.sum(blended * blended)) + epsilon
    iterate = (blended / frob_norm).astype(jnp.bfloat16)
    result = iterate
    for iteration in range(NS_ITERS):
        gram_matrix = lax.dot_general(
            iterate, iterate, (((1,), (1,)), ((), ())), preferred_element_type=jnp.float32
        ).astype(jnp.bfloat16)
        square = jnp.dot(gram_matrix, gram_matrix, preferred_element_type=jnp.float32)
        polynomial = (
            quintic_two * gram_matrix.astype(jnp.float32) + quintic_three * square
        ).astype(jnp.bfloat16)
        next_iter = quintic_one * iterate.astype(jnp.float32) + jnp.dot(
            polynomial, iterate, preferred_element_type=jnp.float32
        )
        if iteration + 1 < NS_ITERS:
            iterate = next_iter.astype(jnp.bfloat16)
        else:
            result = (math.sqrt(extent) * next_iter).astype(jnp.bfloat16)
    return (result, moment_new)


def spare_pair(full_grad, moment):
    return (jnp.zeros(full_grad.shape, jnp.bfloat16), jnp.zeros(moment.shape, jnp.float32))


def body(grad_rows, row_counts, owners, momentum):
    matrices, capacity, extent = grad_rows.shape
    shards = lax.axis_size("dp")
    dp_index = lax.axis_index("dp")
    rep_index = lax.axis_index("rep")
    slot_ids = slots_of(owners)
    matrix_ids = jnp.arange(matrices, dtype=jnp.int32)
    owner_ids = jnp.arange(shards, dtype=jnp.int32)
    in_lane = slot_ids == rep_index
    lane_pick = (owners[None, :] == owner_ids[:, None]) & in_lane[None, :]
    lane_valid = jnp.any(lane_pick, axis=1)
    lane_matrix = jnp.sum(jnp.where(lane_pick, matrix_ids[None, :], 0), axis=1)
    send_table = jnp.take(grad_rows, lane_matrix, axis=0)
    send_table = jnp.where(lane_valid[:, None, None], send_table, jnp.zeros_like(send_table))
    arrived = lax.all_to_all(send_table, "dp", split_axis=0, concat_axis=0, tiled=True)

    held_here = (owners == dp_index) & in_lane
    active = jnp.any(held_here)
    counts = jnp.sum(jnp.where(held_here[:, None], row_counts, 0), axis=0)
    starts = exclusive_starts(counts)
    row_ids = jnp.arange(extent, dtype=jnp.int32)
    covers = (starts[None, :] <= row_ids[:, None]) & (row_ids[:, None] < (starts + counts)[None, :])
    holder = jnp.sum(jnp.where(covers, owner_ids[None, :], 0), axis=1)
    first_row = jnp.sum(jnp.where(covers, starts[None, :], 0), axis=1)
    row_index = holder * capacity + (row_ids - first_row)
    full_grad = jnp.take(arrived.reshape(shards * capacity, extent), row_index, axis=0)
    update, moment_new = lax.cond(active, orthogonalize, spare_pair, full_grad, momentum[0, 0])

    offsets = jnp.arange(capacity, dtype=jnp.int32)
    positions = jnp.clip(starts[:, None] + offsets[None, :], 0, extent - 1)
    usable = offsets[None, :] < counts[:, None]
    outgoing = jnp.take(update, positions.reshape(-1), axis=0).reshape(shards, capacity, extent)
    outgoing = jnp.where(usable[:, :, None], outgoing, jnp.zeros_like(outgoing))
    returned = lax.all_to_all(outgoing, "dp", split_axis=0, concat_axis=0, tiled=True)
    mine = jnp.take(returned, owners, axis=0)
    mine = jnp.where(in_lane[:, None, None], mine, jnp.zeros_like(mine))
    picked_rows = lax.psum(mine, "rep")
    return (picked_rows, moment_new[None, None])


def solution(mesh):
    return jax.shard_map(
        body,
        mesh=mesh,
        in_specs=(P(None, "dp", None), P(), P(), P("dp", "rep", None, None)),
        out_specs=(P(None, "dp", None), P("dp", "rep", None, None)),
        check_vma=False,
    )
```

```python
import math

import jax
import jax.numpy as jnp
from jax import lax
from jax.sharding import PartitionSpec as P

NS_ITERS = 5


momentum_decay = 0.95
grad_share = 0.05
epsilon = 1e-06
quintic_one = 3.4445
quintic_two = -4.775
quintic_three = 2.0315


def slots_of(owners):
    total = owners.shape[0]
    same_owner = owners[:, None] == owners[None, :]
    position = jnp.arange(total, dtype=jnp.int32)
    earlier = position[None, :] < position[:, None]
    return jnp.sum((same_owner & earlier).astype(jnp.int32), axis=1)


def exclusive_starts(counts):
    shards = counts.shape[0]
    ids = jnp.arange(shards, dtype=jnp.int32)
    before = ids[None, :] < ids[:, None]
    return jnp.sum(jnp.where(before, counts[None, :], 0), axis=1)


def orthogonalize(full_grad, moment):
    extent = full_grad.shape[0]
    gradient = full_grad.astype(jnp.float32)
    moment_new = momentum_decay * moment + grad_share * gradient
    blended = grad_share * gradient + momentum_decay * moment_new
    frob_norm = jnp.sqrt(jnp.sum(blended * blended)) + epsilon
    iterate = (blended / frob_norm).astype(jnp.bfloat16)
    result = iterate
    for iteration in range(NS_ITERS):
        gram_matrix = lax.dot_general(
            iterate, iterate, (((1,), (1,)), ((), ())), preferred_element_type=jnp.float32
        ).astype(jnp.bfloat16)
        square = jnp.dot(gram_matrix, gram_matrix, preferred_element_type=jnp.float32)
        polynomial = (
            quintic_two * gram_matrix.astype(jnp.float32) + quintic_three * square
        ).astype(jnp.bfloat16)
        next_iter = quintic_one * iterate.astype(jnp.float32) + jnp.dot(
            polynomial, iterate, preferred_element_type=jnp.float32
        )
        if iteration + 1 < NS_ITERS:
            iterate = next_iter.astype(jnp.bfloat16)
        else:
            result = (math.sqrt(extent) * next_iter).astype(jnp.bfloat16)
    return (result, moment_new)


def spare_pair(full_grad, moment):
    return (jnp.zeros(full_grad.shape, jnp.bfloat16), jnp.zeros(moment.shape, jnp.float32))


def body(grad_rows, row_counts, owners, momentum):
    matrices, capacity, extent = grad_rows.shape
    shards = lax.axis_size("dp")
    dp_index = lax.axis_index("dp")
    rep_index = lax.axis_index("rep")
    slot_ids = slots_of(owners)
    matrix_ids = jnp.arange(matrices, dtype=jnp.int32)
    owner_ids = jnp.arange(shards, dtype=jnp.int32)
    in_lane = slot_ids == rep_index
    lane_pick = (owners[None, :] == owner_ids[:, None]) & in_lane[None, :]
    lane_valid = jnp.any(lane_pick, axis=1)
    lane_matrix = jnp.sum(jnp.where(lane_pick, matrix_ids[None, :], 0), axis=1)
    send_table = jnp.take(grad_rows, lane_matrix, axis=0)
    send_table = jnp.where(lane_valid[:, None, None], send_table, jnp.zeros_like(send_table))
    arrived = lax.all_to_all(send_table, "dp", split_axis=0, concat_axis=0, tiled=True)

    held_here = (owners == dp_index) & in_lane
    active = jnp.any(held_here)
    counts = jnp.sum(jnp.where(held_here[:, None], row_counts, 0), axis=0)
    starts = exclusive_starts(counts)
    row_ids = jnp.arange(extent, dtype=jnp.int32)
    covers = (starts[None, :] <= row_ids[:, None]) & (row_ids[:, None] < (starts + counts)[None, :])
    holder = jnp.sum(jnp.where(covers, owner_ids[None, :], 0), axis=1)
    first_row = jnp.sum(jnp.where(covers, starts[None, :], 0), axis=1)
    row_index = holder * capacity + (row_ids - first_row)
    full_grad = jnp.take(arrived.reshape(shards * capacity, extent), row_index, axis=0)
    update, moment_new = lax.cond(active, orthogonalize, spare_pair, full_grad, momentum[0, 0])

    offsets = jnp.arange(capacity, dtype=jnp.int32)
    positions = jnp.clip(starts[:, None] + offsets[None, :], 0, extent - 1)
    usable = offsets[None, :] < counts[:, None]
    outgoing = jnp.take(update, positions.reshape(-1), axis=0).reshape(shards, capacity, extent)
    outgoing = jnp.where(usable[:, :, None], outgoing, jnp.zeros_like(outgoing))
    lanes = lax.axis_size("rep")
    quarter = capacity // lanes
    outgoing = outgoing.reshape(shards * lanes, quarter, extent)
    returned = lax.all_to_all(outgoing, ("dp", "rep"), split_axis=0, concat_axis=0, tiled=True)
    mine = jnp.take(returned, owners * lanes + slot_ids, axis=0)
    picked_rows = lax.all_gather(mine, "rep", axis=1, tiled=True)
    return (picked_rows, moment_new[None, None])


def solution(mesh):
    return jax.shard_map(
        body,
        mesh=mesh,
        in_specs=(P(None, "dp", None), P(), P(), P("dp", "rep", None, None)),
        out_specs=(P(None, "dp", None), P("dp", "rep", None, None)),
        check_vma=False,
    )
```

```python
import math

import jax
import jax.numpy as jnp
from jax import lax
from jax.experimental import pallas as pl
from jax.experimental.pallas import tpu as pltpu
from jax.sharding import PartitionSpec as P

NS_ITERS = 5


momentum_decay = 0.95
grad_share = 0.05
epsilon = 1e-06
quintic_one = 3.4445
quintic_two = -4.775
quintic_three = 2.0315


def slots_of(owners):
    total = owners.shape[0]
    same_owner = owners[:, None] == owners[None, :]
    position = jnp.arange(total, dtype=jnp.int32)
    earlier = position[None, :] < position[:, None]
    return jnp.sum((same_owner & earlier).astype(jnp.int32), axis=1)


def exclusive_starts(counts):
    shards = counts.shape[0]
    ids = jnp.arange(shards, dtype=jnp.int32)
    before = ids[None, :] < ids[:, None]
    return jnp.sum(jnp.where(before, counts[None, :], 0), axis=1)


def orthogonalize(full_grad, moment):
    extent = full_grad.shape[0]
    gradient = full_grad.astype(jnp.float32)
    moment_new = momentum_decay * moment + grad_share * gradient
    blended = grad_share * gradient + momentum_decay * moment_new
    frob_norm = jnp.sqrt(jnp.sum(blended * blended)) + epsilon
    iterate = (blended / frob_norm).astype(jnp.bfloat16)
    result = iterate
    for iteration in range(NS_ITERS):
        gram_matrix = lax.dot_general(
            iterate, iterate, (((1,), (1,)), ((), ())), preferred_element_type=jnp.float32
        ).astype(jnp.bfloat16)
        square = jnp.dot(gram_matrix, gram_matrix, preferred_element_type=jnp.float32)
        polynomial = (
            quintic_two * gram_matrix.astype(jnp.float32) + quintic_three * square
        ).astype(jnp.bfloat16)
        next_iter = quintic_one * iterate.astype(jnp.float32) + jnp.dot(
            polynomial, iterate, preferred_element_type=jnp.float32
        )
        if iteration + 1 < NS_ITERS:
            iterate = next_iter.astype(jnp.bfloat16)
        else:
            result = (math.sqrt(extent) * next_iter).astype(jnp.bfloat16)
    return (result, moment_new)


TILE = 256
TRANSPOSED = (((1,), (1,)), ((), ()))


def newton_schulz_kernel(g_ref, m_ref, u_ref, mn_ref, x0_ref, x1_ref, a_ref, p_ref):
    extent = g_ref.shape[0]
    tiles = extent // TILE

    def rows_of(i):
        return pl.ds(pl.multiple_of(i * TILE, TILE), TILE)

    def moment_tile(i, acc):
        rows = rows_of(i)
        gradient = g_ref[rows, :].astype(jnp.float32)
        moment_new = momentum_decay * m_ref[rows, :] + grad_share * gradient
        mn_ref[rows, :] = moment_new
        blended = grad_share * gradient + momentum_decay * moment_new
        return acc + jnp.sum(blended * blended, axis=0, keepdims=True)

    acc = lax.fori_loop(0, tiles, moment_tile, jnp.zeros((1, extent), jnp.float32))
    frob_norm = jnp.sqrt(jnp.sum(acc, axis=1, keepdims=True)) + epsilon

    def scale_tile(i, carry):
        rows = rows_of(i)
        gradient = g_ref[rows, :].astype(jnp.float32)
        blended = grad_share * gradient + momentum_decay * mn_ref[rows, :]
        x0_ref[rows, :] = (blended / frob_norm).astype(jnp.bfloat16)
        return carry

    lax.fori_loop(0, tiles, scale_tile, 0)
    iterates = (x0_ref, x1_ref)
    for iteration in range(NS_ITERS):
        now = iterates[iteration % 2]
        later = iterates[(iteration + 1) % 2]
        last = iteration + 1 == NS_ITERS

        def gram_tile(i, carry, now=now):
            rows = rows_of(i)
            a_ref[rows, :] = lax.dot_general(
                now[rows, :], now[...], TRANSPOSED, preferred_element_type=jnp.float32
            ).astype(jnp.bfloat16)
            return carry

        def poly_tile(i, carry):
            rows = rows_of(i)
            gram_rows = a_ref[rows, :]
            square = jnp.dot(gram_rows, a_ref[...], preferred_element_type=jnp.float32)
            p_ref[rows, :] = (
                quintic_two * gram_rows.astype(jnp.float32) + quintic_three * square
            ).astype(jnp.bfloat16)
            return carry

        def next_tile(i, carry, now=now, later=later, last=last):
            rows = rows_of(i)
            next_iter = quintic_one * now[rows, :].astype(jnp.float32) + jnp.dot(
                p_ref[rows, :], now[...], preferred_element_type=jnp.float32
            )
            if last:
                u_ref[rows, :] = (math.sqrt(extent) * next_iter).astype(jnp.bfloat16)
            else:
                later[rows, :] = next_iter.astype(jnp.bfloat16)
            return carry

        lax.fori_loop(0, tiles, gram_tile, 0)
        lax.fori_loop(0, tiles, poly_tile, 0)
        lax.fori_loop(0, tiles, next_tile, 0)


def orthogonalize_kernel(full_grad, moment):
    extent = full_grad.shape[0]
    square = (extent, extent)
    vmem = pl.BlockSpec(memory_space=pltpu.VMEM)
    return pl.pallas_call(
        newton_schulz_kernel,
        out_shape=(
            jax.ShapeDtypeStruct(square, jnp.bfloat16),
            jax.ShapeDtypeStruct(square, jnp.float32),
        ),
        in_specs=[vmem, vmem],
        out_specs=(vmem, vmem),
        scratch_shapes=[pltpu.VMEM(square, jnp.bfloat16) for _ in range(4)],
        compiler_params=pltpu.CompilerParams(vmem_limit_bytes=48 * 1024 * 1024),
        cost_estimate=pl.CostEstimate(
            flops=2 * 3 * NS_ITERS * extent ** 3,
            bytes_accessed=12 * extent * extent,
            transcendentals=0,
        ),
    )(full_grad, moment)


def spare_pair(full_grad, moment):
    return (jnp.zeros(full_grad.shape, jnp.bfloat16), jnp.zeros(moment.shape, jnp.float32))


def body(grad_rows, row_counts, owners, momentum):
    matrices, capacity, extent = grad_rows.shape
    shards = lax.axis_size("dp")
    dp_index = lax.axis_index("dp")
    rep_index = lax.axis_index("rep")
    slot_ids = slots_of(owners)
    matrix_ids = jnp.arange(matrices, dtype=jnp.int32)
    owner_ids = jnp.arange(shards, dtype=jnp.int32)
    in_lane = slot_ids == rep_index
    lane_pick = (owners[None, :] == owner_ids[:, None]) & in_lane[None, :]
    lane_valid = jnp.any(lane_pick, axis=1)
    lane_matrix = jnp.sum(jnp.where(lane_pick, matrix_ids[None, :], 0), axis=1)
    send_table = jnp.take(grad_rows, lane_matrix, axis=0)
    send_table = jnp.where(lane_valid[:, None, None], send_table, jnp.zeros_like(send_table))
    arrived = lax.all_to_all(send_table, "dp", split_axis=0, concat_axis=0, tiled=True)

    held_here = (owners == dp_index) & in_lane
    active = jnp.any(held_here)
    counts = jnp.sum(jnp.where(held_here[:, None], row_counts, 0), axis=0)
    starts = exclusive_starts(counts)
    row_ids = jnp.arange(extent, dtype=jnp.int32)
    covers = (starts[None, :] <= row_ids[:, None]) & (row_ids[:, None] < (starts + counts)[None, :])
    holder = jnp.sum(jnp.where(covers, owner_ids[None, :], 0), axis=1)
    first_row = jnp.sum(jnp.where(covers, starts[None, :], 0), axis=1)
    row_index = holder * capacity + (row_ids - first_row)
    full_grad = jnp.take(arrived.reshape(shards * capacity, extent), row_index, axis=0)
    update, moment_new = lax.cond(active, orthogonalize_kernel, spare_pair, full_grad, momentum[0, 0])

    offsets = jnp.arange(capacity, dtype=jnp.int32)
    positions = jnp.clip(starts[:, None] + offsets[None, :], 0, extent - 1)
    usable = offsets[None, :] < counts[:, None]
    outgoing = jnp.take(update, positions.reshape(-1), axis=0).reshape(shards, capacity, extent)
    outgoing = jnp.where(usable[:, :, None], outgoing, jnp.zeros_like(outgoing))
    lanes = lax.axis_size("rep")
    quarter = capacity // lanes
    outgoing = outgoing.reshape(shards * lanes, quarter, extent)
    returned = lax.all_to_all(outgoing, ("dp", "rep"), split_axis=0, concat_axis=0, tiled=True)
    mine = jnp.take(returned, owners * lanes + slot_ids, axis=0)
    picked_rows = lax.all_gather(mine, "rep", axis=1, tiled=True)
    return (picked_rows, moment_new[None, None])


def solution(mesh):
    return jax.shard_map(
        body,
        mesh=mesh,
        in_specs=(P(None, "dp", None), P(), P(), P("dp", "rep", None, None)),
        out_specs=(P(None, "dp", None), P("dp", "rep", None, None)),
        check_vma=False,
    )
```

```python
import math

import jax
import jax.numpy as jnp
from jax import lax
from jax.experimental import pallas as pl
from jax.experimental.pallas import tpu as pltpu
from jax.sharding import PartitionSpec as P

NS_ITERS = 5


momentum_decay = 0.95
grad_share = 0.05
epsilon = 1e-06
quintic_one = 3.4445
quintic_two = -4.775
quintic_three = 2.0315


def slots_of(owners):
    total = owners.shape[0]
    same_owner = owners[:, None] == owners[None, :]
    position = jnp.arange(total, dtype=jnp.int32)
    earlier = position[None, :] < position[:, None]
    return jnp.sum((same_owner & earlier).astype(jnp.int32), axis=1)


def exclusive_starts(counts):
    shards = counts.shape[0]
    ids = jnp.arange(shards, dtype=jnp.int32)
    before = ids[None, :] < ids[:, None]
    return jnp.sum(jnp.where(before, counts[None, :], 0), axis=1)


def orthogonalize(full_grad, moment):
    extent = full_grad.shape[0]
    gradient = full_grad.astype(jnp.float32)
    moment_new = momentum_decay * moment + grad_share * gradient
    blended = grad_share * gradient + momentum_decay * moment_new
    frob_norm = jnp.sqrt(jnp.sum(blended * blended)) + epsilon
    iterate = (blended / frob_norm).astype(jnp.bfloat16)
    result = iterate
    for iteration in range(NS_ITERS):
        gram_matrix = lax.dot_general(
            iterate, iterate, (((1,), (1,)), ((), ())), preferred_element_type=jnp.float32
        ).astype(jnp.bfloat16)
        square = jnp.dot(gram_matrix, gram_matrix, preferred_element_type=jnp.float32)
        polynomial = (
            quintic_two * gram_matrix.astype(jnp.float32) + quintic_three * square
        ).astype(jnp.bfloat16)
        next_iter = quintic_one * iterate.astype(jnp.float32) + jnp.dot(
            polynomial, iterate, preferred_element_type=jnp.float32
        )
        if iteration + 1 < NS_ITERS:
            iterate = next_iter.astype(jnp.bfloat16)
        else:
            result = (math.sqrt(extent) * next_iter).astype(jnp.bfloat16)
    return (result, moment_new)


TILE = 256
TRANSPOSED = (((1,), (1,)), ((), ()))


def newton_schulz_kernel(
    slots_ref, take_ref, m_ref, place_ref, out_ref, mn_ref, g_ref, x0_ref, x1_ref, a_ref, p_ref
):
    extent = g_ref.shape[0]
    tiles = extent // TILE
    slot_total = slots_ref.shape[0]

    def rows_of(i):
        return pl.ds(pl.multiple_of(i * TILE, TILE), TILE)

    def compact_tile(i, carry):
        rows = rows_of(i)
        lanes = lax.broadcasted_iota(jnp.int32, (TILE, slot_total), 1)
        chosen = (take_ref[rows, :] == lanes).astype(jnp.bfloat16)
        g_ref[rows, :] = jnp.dot(
            chosen, slots_ref[...], preferred_element_type=jnp.float32
        ).astype(jnp.bfloat16)
        return carry

    lax.fori_loop(0, tiles, compact_tile, 0)

    def moment_tile(i, acc):
        rows = rows_of(i)
        gradient = g_ref[rows, :].astype(jnp.float32)
        moment_new = momentum_decay * m_ref[rows, :] + grad_share * gradient
        mn_ref[rows, :] = moment_new
        blended = grad_share * gradient + momentum_decay * moment_new
        return acc + jnp.sum(blended * blended, axis=0, keepdims=True)

    acc = lax.fori_loop(0, tiles, moment_tile, jnp.zeros((1, extent), jnp.float32))
    frob_norm = jnp.sqrt(jnp.sum(acc, axis=1, keepdims=True)) + epsilon

    def scale_tile(i, carry):
        rows = rows_of(i)
        gradient = g_ref[rows, :].astype(jnp.float32)
        blended = grad_share * gradient + momentum_decay * mn_ref[rows, :]
        x0_ref[rows, :] = (blended / frob_norm).astype(jnp.bfloat16)
        return carry

    lax.fori_loop(0, tiles, scale_tile, 0)
    iterates = (x0_ref, x1_ref)
    for iteration in range(NS_ITERS):
        now = iterates[iteration % 2]
        later = iterates[(iteration + 1) % 2]
        last = iteration + 1 == NS_ITERS

        def gram_tile(i, carry, now=now):
            rows = rows_of(i)
            a_ref[rows, :] = lax.dot_general(
                now[rows, :], now[...], TRANSPOSED, preferred_element_type=jnp.float32
            ).astype(jnp.bfloat16)
            return carry

        def poly_tile(i, carry):
            rows = rows_of(i)
            gram_rows = a_ref[rows, :]
            square = jnp.dot(gram_rows, a_ref[...], preferred_element_type=jnp.float32)
            p_ref[rows, :] = (
                quintic_two * gram_rows.astype(jnp.float32) + quintic_three * square
            ).astype(jnp.bfloat16)
            return carry

        def next_tile(i, carry, now=now, later=later, last=last):
            rows = rows_of(i)
            next_iter = quintic_one * now[rows, :].astype(jnp.float32) + jnp.dot(
                p_ref[rows, :], now[...], preferred_element_type=jnp.float32
            )
            if last:
                a_ref[rows, :] = (math.sqrt(extent) * next_iter).astype(jnp.bfloat16)
            else:
                later[rows, :] = next_iter.astype(jnp.bfloat16)
            return carry

        lax.fori_loop(0, tiles, gram_tile, 0)
        lax.fori_loop(0, tiles, poly_tile, 0)
        lax.fori_loop(0, tiles, next_tile, 0)

    def place_tile(i, carry):
        rows = rows_of(i)
        lanes = lax.broadcasted_iota(jnp.int32, (TILE, extent), 1)
        chosen = (place_ref[rows, :] == lanes).astype(jnp.bfloat16)
        out_ref[rows, :] = jnp.dot(
            chosen, a_ref[...], preferred_element_type=jnp.float32
        ).astype(jnp.bfloat16)
        return carry

    lax.fori_loop(0, slot_total // TILE, place_tile, 0)


def orthogonalize_kernel(slots, take, moment, place):
    extent = moment.shape[0]
    square = (extent, extent)
    vmem = pl.BlockSpec(memory_space=pltpu.VMEM)
    return pl.pallas_call(
        newton_schulz_kernel,
        out_shape=(
            jax.ShapeDtypeStruct(slots.shape, jnp.bfloat16),
            jax.ShapeDtypeStruct(square, jnp.float32),
        ),
        in_specs=[vmem, vmem, vmem, vmem],
        out_specs=(vmem, vmem),
        scratch_shapes=[pltpu.VMEM(square, jnp.bfloat16) for _ in range(5)],
        compiler_params=pltpu.CompilerParams(vmem_limit_bytes=48 * 1024 * 1024),
        cost_estimate=pl.CostEstimate(
            flops=2 * (3 * NS_ITERS + 2) * extent ** 3,
            bytes_accessed=16 * extent * extent,
            transcendentals=0,
        ),
    )(slots, take, moment, place)


def spare_pair(slots, take, moment, place):
    return (jnp.zeros(slots.shape, jnp.bfloat16), jnp.zeros(moment.shape, jnp.float32))


def body(grad_rows, row_counts, owners, momentum):
    matrices, capacity, extent = grad_rows.shape
    shards = lax.axis_size("dp")
    dp_index = lax.axis_index("dp")
    rep_index = lax.axis_index("rep")
    slot_ids = slots_of(owners)
    matrix_ids = jnp.arange(matrices, dtype=jnp.int32)
    owner_ids = jnp.arange(shards, dtype=jnp.int32)
    in_lane = slot_ids == rep_index
    lane_pick = (owners[None, :] == owner_ids[:, None]) & in_lane[None, :]
    lane_valid = jnp.any(lane_pick, axis=1)
    lane_matrix = jnp.sum(jnp.where(lane_pick, matrix_ids[None, :], 0), axis=1)
    send_table = jnp.take(grad_rows, lane_matrix, axis=0)
    send_table = jnp.where(lane_valid[:, None, None], send_table, jnp.zeros_like(send_table))
    arrived = lax.all_to_all(send_table, "dp", split_axis=0, concat_axis=0, tiled=True)

    held_here = (owners == dp_index) & in_lane
    active = jnp.any(held_here)
    counts = jnp.sum(jnp.where(held_here[:, None], row_counts, 0), axis=0)
    starts = exclusive_starts(counts)
    row_ids = jnp.arange(extent, dtype=jnp.int32)
    covers = (starts[None, :] <= row_ids[:, None]) & (row_ids[:, None] < (starts + counts)[None, :])
    holder = jnp.sum(jnp.where(covers, owner_ids[None, :], 0), axis=1)
    first_row = jnp.sum(jnp.where(covers, starts[None, :], 0), axis=1)
    row_index = holder * capacity + (row_ids - first_row)
    offsets = jnp.arange(capacity, dtype=jnp.int32)
    positions = starts[:, None] + offsets[None, :]
    usable = offsets[None, :] < counts[:, None]
    place = jnp.where(usable, positions, -1).reshape(shards * capacity, 1)
    outgoing, moment_new = lax.cond(
        active,
        orthogonalize_kernel,
        spare_pair,
        arrived.reshape(shards * capacity, extent),
        row_index[:, None],
        momentum[0, 0],
        place,
    )
    lanes = lax.axis_size("rep")
    quarter = capacity // lanes
    outgoing = outgoing.reshape(shards * lanes, quarter, extent)
    returned = lax.all_to_all(outgoing, ("dp", "rep"), split_axis=0, concat_axis=0, tiled=True)
    mine = jnp.take(returned, owners * lanes + slot_ids, axis=0)
    picked_rows = lax.all_gather(mine, "rep", axis=1, tiled=True)
    return (picked_rows, moment_new[None, None])


def solution(mesh):
    return jax.shard_map(
        body,
        mesh=mesh,
        in_specs=(P(None, "dp", None), P(), P(), P("dp", "rep", None, None)),
        out_specs=(P(None, "dp", None), P("dp", "rep", None, None)),
        check_vma=False,
    )
```

```python
import math

import jax
import jax.numpy as jnp
from jax import lax
from jax.experimental import pallas as pl
from jax.experimental.pallas import tpu as pltpu
from jax.sharding import PartitionSpec as P

NS_ITERS = 5


momentum_decay = 0.95
grad_share = 0.05
epsilon = 1e-06
quintic_one = 3.4445
quintic_two = -4.775
quintic_three = 2.0315


def slots_of(owners):
    total = owners.shape[0]
    same_owner = owners[:, None] == owners[None, :]
    position = jnp.arange(total, dtype=jnp.int32)
    earlier = position[None, :] < position[:, None]
    return jnp.sum((same_owner & earlier).astype(jnp.int32), axis=1)


def exclusive_starts(counts):
    shards = counts.shape[0]
    ids = jnp.arange(shards, dtype=jnp.int32)
    before = ids[None, :] < ids[:, None]
    return jnp.sum(jnp.where(before, counts[None, :], 0), axis=1)


def orthogonalize(full_grad, moment):
    extent = full_grad.shape[0]
    gradient = full_grad.astype(jnp.float32)
    moment_new = momentum_decay * moment + grad_share * gradient
    blended = grad_share * gradient + momentum_decay * moment_new
    frob_norm = jnp.sqrt(jnp.sum(blended * blended)) + epsilon
    iterate = (blended / frob_norm).astype(jnp.bfloat16)
    result = iterate
    for iteration in range(NS_ITERS):
        gram_matrix = lax.dot_general(
            iterate, iterate, (((1,), (1,)), ((), ())), preferred_element_type=jnp.float32
        ).astype(jnp.bfloat16)
        square = jnp.dot(gram_matrix, gram_matrix, preferred_element_type=jnp.float32)
        polynomial = (
            quintic_two * gram_matrix.astype(jnp.float32) + quintic_three * square
        ).astype(jnp.bfloat16)
        next_iter = quintic_one * iterate.astype(jnp.float32) + jnp.dot(
            polynomial, iterate, preferred_element_type=jnp.float32
        )
        if iteration + 1 < NS_ITERS:
            iterate = next_iter.astype(jnp.bfloat16)
        else:
            result = (math.sqrt(extent) * next_iter).astype(jnp.bfloat16)
    return (result, moment_new)


TILE = 256
TRANSPOSED = (((1,), (1,)), ((), ()))


def newton_schulz_kernel(
    slots_ref, take_ref, m_ref, place_ref, out_ref, mn_ref, g_ref, x0_ref, x1_ref, a_ref, p_ref
):
    extent = g_ref.shape[0]
    tiles = extent // TILE
    slot_total = slots_ref.shape[0]

    def rows_of(i):
        return pl.ds(pl.multiple_of(i * TILE, TILE), TILE)

    def compact_tile(i, carry):
        rows = rows_of(i)
        lanes = lax.broadcasted_iota(jnp.int32, (TILE, slot_total), 1)
        chosen = (take_ref[rows, :] == lanes).astype(jnp.bfloat16)
        g_ref[rows, :] = jnp.dot(
            chosen, slots_ref[...], preferred_element_type=jnp.float32
        ).astype(jnp.bfloat16)
        return carry

    lax.fori_loop(0, tiles, compact_tile, 0)

    def moment_tile(i, acc):
        rows = rows_of(i)
        gradient = g_ref[rows, :].astype(jnp.float32)
        moment_new = momentum_decay * m_ref[rows, :] + grad_share * gradient
        mn_ref[rows, :] = moment_new
        blended = grad_share * gradient + momentum_decay * moment_new
        return acc + jnp.sum(blended * blended, axis=0, keepdims=True)

    acc = lax.fori_loop(0, tiles, moment_tile, jnp.zeros((1, extent), jnp.float32))
    frob_norm = jnp.sqrt(jnp.sum(acc, axis=1, keepdims=True)) + epsilon

    def scale_tile(i, carry):
        rows = rows_of(i)
        gradient = g_ref[rows, :].astype(jnp.float32)
        blended = grad_share * gradient + momentum_decay * mn_ref[rows, :]
        x0_ref[rows, :] = (blended / frob_norm).astype(jnp.bfloat16)
        return carry

    lax.fori_loop(0, tiles, scale_tile, 0)
    iterates = (x0_ref, x1_ref)
    for iteration in range(NS_ITERS):
        now = iterates[iteration % 2]
        later = iterates[(iteration + 1) % 2]
        last = iteration + 1 == NS_ITERS

        def gram_tile(i, carry, now=now):
            rows = rows_of(i)
            a_ref[rows, :] = lax.dot_general(
                now[rows, :], now[...], TRANSPOSED, preferred_element_type=jnp.float32
            ).astype(jnp.bfloat16)
            return carry

        def poly_tile(i, carry):
            rows = rows_of(i)
            gram_rows = a_ref[rows, :]
            square = jnp.dot(gram_rows, a_ref[...], preferred_element_type=jnp.float32)
            p_ref[rows, :] = (
                quintic_two * gram_rows.astype(jnp.float32) + quintic_three * square
            ).astype(jnp.bfloat16)
            return carry

        def next_tile(i, carry, now=now, later=later, last=last):
            rows = rows_of(i)
            next_iter = quintic_one * now[rows, :].astype(jnp.float32) + jnp.dot(
                p_ref[rows, :], now[...], preferred_element_type=jnp.float32
            )
            if last:
                a_ref[rows, :] = (math.sqrt(extent) * next_iter).astype(jnp.bfloat16)
            else:
                later[rows, :] = next_iter.astype(jnp.bfloat16)
            return carry

        lax.fori_loop(0, tiles, gram_tile, 0)
        lax.fori_loop(0, tiles, poly_tile, 0)
        lax.fori_loop(0, tiles, next_tile, 0)

    def place_tile(i, carry):
        rows = rows_of(i)
        lanes = lax.broadcasted_iota(jnp.int32, (TILE, extent), 1)
        chosen = (place_ref[rows, :] == lanes).astype(jnp.bfloat16)
        out_ref[rows, :] = jnp.dot(
            chosen, a_ref[...], preferred_element_type=jnp.float32
        ).astype(jnp.bfloat16)
        return carry

    lax.fori_loop(0, slot_total // TILE, place_tile, 0)


def orthogonalize_kernel(slots, take, moment, place):
    extent = moment.shape[0]
    square = (extent, extent)
    vmem = pl.BlockSpec(memory_space=pltpu.VMEM)
    return pl.pallas_call(
        newton_schulz_kernel,
        out_shape=(
            jax.ShapeDtypeStruct(slots.shape, jnp.bfloat16),
            jax.ShapeDtypeStruct(square, jnp.float32),
        ),
        in_specs=[vmem, vmem, vmem, vmem],
        out_specs=(vmem, vmem),
        scratch_shapes=[pltpu.VMEM(square, jnp.bfloat16) for _ in range(5)],
        compiler_params=pltpu.CompilerParams(vmem_limit_bytes=48 * 1024 * 1024),
        cost_estimate=pl.CostEstimate(
            flops=2 * (3 * NS_ITERS + 2) * extent ** 3,
            bytes_accessed=16 * extent * extent,
            transcendentals=0,
        ),
    )(slots, take, moment, place)


def spare_pair(slots, take, moment, place):
    return (jnp.zeros(slots.shape, jnp.bfloat16), jnp.zeros(moment.shape, jnp.float32))


def body(grad_rows, row_counts, owners, momentum):
    matrices, capacity, extent = grad_rows.shape
    shards = lax.axis_size("dp")
    dp_index = lax.axis_index("dp")
    rep_index = lax.axis_index("rep")
    slot_ids = slots_of(owners)
    matrix_ids = jnp.arange(matrices, dtype=jnp.int32)
    owner_ids = jnp.arange(shards, dtype=jnp.int32)
    in_lane = slot_ids == rep_index
    lane_pick = (owners[None, :] == owner_ids[:, None]) & in_lane[None, :]
    lane_valid = jnp.any(lane_pick, axis=1)
    lane_matrix = jnp.sum(jnp.where(lane_pick, matrix_ids[None, :], 0), axis=1)
    send_table = jnp.take(grad_rows, lane_matrix, axis=0)
    send_table = jnp.where(lane_valid[:, None, None], send_table, jnp.zeros_like(send_table))
    arrived = lax.all_to_all(send_table, "dp", split_axis=0, concat_axis=0, tiled=True)

    held_here = (owners == dp_index) & in_lane
    active = jnp.any(held_here)
    counts = jnp.sum(jnp.where(held_here[:, None], row_counts, 0), axis=0)
    starts = exclusive_starts(counts)
    row_ids = jnp.arange(extent, dtype=jnp.int32)
    covers = (starts[None, :] <= row_ids[:, None]) & (row_ids[:, None] < (starts + counts)[None, :])
    holder = jnp.sum(jnp.where(covers, owner_ids[None, :], 0), axis=1)
    first_row = jnp.sum(jnp.where(covers, starts[None, :], 0), axis=1)
    row_index = holder * capacity + (row_ids - first_row)
    offsets = jnp.arange(capacity, dtype=jnp.int32)
    positions = starts[:, None] + offsets[None, :]
    usable = offsets[None, :] < counts[:, None]
    place = jnp.where(usable, positions, -1).reshape(shards * capacity, 1)
    outgoing, moment_new = lax.cond(
        active,
        orthogonalize_kernel,
        spare_pair,
        arrived.reshape(shards * capacity, extent),
        row_index[:, None],
        momentum[0, 0],
        place,
    )
    lanes = lax.axis_size("rep")
    quarter = capacity // lanes
    outgoing = outgoing.reshape(shards * lanes, quarter, extent)
    returned = lax.all_to_all(outgoing, ("dp", "rep"), split_axis=0, concat_axis=0, tiled=True)
    mine = jnp.take(returned, owners * lanes + slot_ids, axis=0)
    picked_rows = jnp.zeros((matrices, capacity, extent), mine.dtype)
    for shift in range(lanes):
        if shift == 0:
            block = mine
        else:
            block = lax.ppermute(mine, "rep", [(q, (q + shift) % lanes) for q in range(lanes)])
        source = (rep_index - shift + lanes) % lanes
        picked_rows = lax.dynamic_update_slice(picked_rows, block, (0, source * quarter, 0))
    return (picked_rows, moment_new[None, None])


def solution(mesh):
    return jax.shard_map(
        body,
        mesh=mesh,
        in_specs=(P(None, "dp", None), P(), P(), P("dp", "rep", None, None)),
        out_specs=(P(None, "dp", None), P("dp", "rep", None, None)),
        check_vma=False,
    )
```

```python
import math

import jax
import jax.numpy as jnp
from jax import lax
from jax.experimental import pallas as pl
from jax.experimental.pallas import tpu as pltpu
from jax.sharding import PartitionSpec as P

NS_ITERS = 5


momentum_decay = 0.95
grad_share = 0.05
epsilon = 1e-06
quintic_one = 3.4445
quintic_two = -4.775
quintic_three = 2.0315


def slots_of(owners):
    total = owners.shape[0]
    same_owner = owners[:, None] == owners[None, :]
    position = jnp.arange(total, dtype=jnp.int32)
    earlier = position[None, :] < position[:, None]
    return jnp.sum((same_owner & earlier).astype(jnp.int32), axis=1)


def exclusive_starts(counts):
    shards = counts.shape[0]
    ids = jnp.arange(shards, dtype=jnp.int32)
    before = ids[None, :] < ids[:, None]
    return jnp.sum(jnp.where(before, counts[None, :], 0), axis=1)


def orthogonalize(full_grad, moment):
    extent = full_grad.shape[0]
    gradient = full_grad.astype(jnp.float32)
    moment_new = momentum_decay * moment + grad_share * gradient
    blended = grad_share * gradient + momentum_decay * moment_new
    frob_norm = jnp.sqrt(jnp.sum(blended * blended)) + epsilon
    iterate = (blended / frob_norm).astype(jnp.bfloat16)
    result = iterate
    for iteration in range(NS_ITERS):
        gram_matrix = lax.dot_general(
            iterate, iterate, (((1,), (1,)), ((), ())), preferred_element_type=jnp.float32
        ).astype(jnp.bfloat16)
        square = jnp.dot(gram_matrix, gram_matrix, preferred_element_type=jnp.float32)
        polynomial = (
            quintic_two * gram_matrix.astype(jnp.float32) + quintic_three * square
        ).astype(jnp.bfloat16)
        next_iter = quintic_one * iterate.astype(jnp.float32) + jnp.dot(
            polynomial, iterate, preferred_element_type=jnp.float32
        )
        if iteration + 1 < NS_ITERS:
            iterate = next_iter.astype(jnp.bfloat16)
        else:
            result = (math.sqrt(extent) * next_iter).astype(jnp.bfloat16)
    return (result, moment_new)


TILE = 256
TRANSPOSED = (((1,), (1,)), ((), ()))


def newton_schulz_kernel(
    slots_ref, take_ref, m_ref, place_ref, out_ref, mn_ref, g_ref, x0_ref, x1_ref, a_ref, p_ref
):
    extent = g_ref.shape[0]
    tiles = extent // TILE
    slot_total = slots_ref.shape[0]

    def rows_of(i):
        return pl.ds(pl.multiple_of(i * TILE, TILE), TILE)

    def compact_tile(i, carry):
        rows = rows_of(i)
        lanes = lax.broadcasted_iota(jnp.int32, (TILE, slot_total), 1)
        chosen = (take_ref[rows, :] == lanes).astype(jnp.bfloat16)
        g_ref[rows, :] = jnp.dot(
            chosen, slots_ref[...], preferred_element_type=jnp.float32
        ).astype(jnp.bfloat16)
        return carry

    lax.fori_loop(0, tiles, compact_tile, 0)

    def moment_tile(i, acc):
        rows = rows_of(i)
        gradient = g_ref[rows, :].astype(jnp.float32)
        moment_new = momentum_decay * m_ref[rows, :] + grad_share * gradient
        mn_ref[rows, :] = moment_new
        blended = grad_share * gradient + momentum_decay * moment_new
        return acc + jnp.sum(blended * blended, axis=0, keepdims=True)

    acc = lax.fori_loop(0, tiles, moment_tile, jnp.zeros((1, extent), jnp.float32))
    frob_norm = jnp.sqrt(jnp.sum(acc, axis=1, keepdims=True)) + epsilon

    def scale_tile(i, carry):
        rows = rows_of(i)
        gradient = g_ref[rows, :].astype(jnp.float32)
        blended = grad_share * gradient + momentum_decay * mn_ref[rows, :]
        x0_ref[rows, :] = (blended / frob_norm).astype(jnp.bfloat16)
        return carry

    lax.fori_loop(0, tiles, scale_tile, 0)
    iterates = (x0_ref, x1_ref)
    for iteration in range(NS_ITERS):
        now = iterates[iteration % 2]
        later = iterates[(iteration + 1) % 2]
        last = iteration + 1 == NS_ITERS

        def gram_tile(i, carry, now=now):
            rows = rows_of(i)
            a_ref[rows, :] = lax.dot_general(
                now[rows, :], now[...], TRANSPOSED, preferred_element_type=jnp.float32
            ).astype(jnp.bfloat16)
            return carry

        def poly_tile(i, carry):
            rows = rows_of(i)
            gram_rows = a_ref[rows, :]
            square = jnp.dot(gram_rows, a_ref[...], preferred_element_type=jnp.float32)
            p_ref[rows, :] = (
                quintic_two * gram_rows.astype(jnp.float32) + quintic_three * square
            ).astype(jnp.bfloat16)
            return carry

        def next_tile(i, carry, now=now, later=later, last=last):
            rows = rows_of(i)
            next_iter = quintic_one * now[rows, :].astype(jnp.float32) + jnp.dot(
                p_ref[rows, :], now[...], preferred_element_type=jnp.float32
            )
            if last:
                a_ref[rows, :] = (math.sqrt(extent) * next_iter).astype(jnp.bfloat16)
            else:
                later[rows, :] = next_iter.astype(jnp.bfloat16)
            return carry

        lax.fori_loop(0, tiles, gram_tile, 0)
        lax.fori_loop(0, tiles, poly_tile, 0)
        lax.fori_loop(0, tiles, next_tile, 0)

    def place_tile(i, carry):
        rows = rows_of(i)
        lanes = lax.broadcasted_iota(jnp.int32, (TILE, extent), 1)
        chosen = (place_ref[rows, :] == lanes).astype(jnp.bfloat16)
        out_ref[rows, :] = jnp.dot(
            chosen, a_ref[...], preferred_element_type=jnp.float32
        ).astype(jnp.bfloat16)
        return carry

    lax.fori_loop(0, slot_total // TILE, place_tile, 0)


def orthogonalize_kernel(slots, take, moment, place):
    extent = moment.shape[0]
    square = (extent, extent)
    vmem = pl.BlockSpec(memory_space=pltpu.VMEM)
    return pl.pallas_call(
        newton_schulz_kernel,
        out_shape=(
            jax.ShapeDtypeStruct(slots.shape, jnp.bfloat16),
            jax.ShapeDtypeStruct(square, jnp.float32),
        ),
        in_specs=[vmem, vmem, vmem, vmem],
        out_specs=(vmem, vmem),
        scratch_shapes=[pltpu.VMEM(square, jnp.bfloat16) for _ in range(5)],
        compiler_params=pltpu.CompilerParams(vmem_limit_bytes=48 * 1024 * 1024),
        cost_estimate=pl.CostEstimate(
            flops=2 * (3 * NS_ITERS + 2) * extent ** 3,
            bytes_accessed=16 * extent * extent,
            transcendentals=0,
        ),
    )(slots, take, moment, place)


def spare_pair(slots, take, moment, place):
    return (jnp.zeros(slots.shape, jnp.bfloat16), jnp.zeros(moment.shape, jnp.float32))


def body(grad_rows, row_counts, owners, momentum):
    matrices, capacity, extent = grad_rows.shape
    shards = lax.axis_size("dp")
    dp_index = lax.axis_index("dp")
    rep_index = lax.axis_index("rep")
    slot_ids = slots_of(owners)
    matrix_ids = jnp.arange(matrices, dtype=jnp.int32)
    owner_ids = jnp.arange(shards, dtype=jnp.int32)
    in_lane = slot_ids == rep_index
    lane_pick = (owners[None, :] == owner_ids[:, None]) & in_lane[None, :]
    lane_matrix = jnp.sum(jnp.where(lane_pick, matrix_ids[None, :], 0), axis=1)
    send_table = jnp.take(grad_rows, lane_matrix, axis=0)
    arrived = lax.all_to_all(send_table, "dp", split_axis=0, concat_axis=0, tiled=True)

    held_here = (owners == dp_index) & in_lane
    active = jnp.any(held_here)
    counts = jnp.sum(jnp.where(held_here[:, None], row_counts, 0), axis=0)
    starts = exclusive_starts(counts)
    row_ids = jnp.arange(extent, dtype=jnp.int32)
    covers = (starts[None, :] <= row_ids[:, None]) & (row_ids[:, None] < (starts + counts)[None, :])
    holder = jnp.sum(jnp.where(covers, owner_ids[None, :], 0), axis=1)
    first_row = jnp.sum(jnp.where(covers, starts[None, :], 0), axis=1)
    row_index = holder * capacity + (row_ids - first_row)
    offsets = jnp.arange(capacity, dtype=jnp.int32)
    positions = starts[:, None] + offsets[None, :]
    usable = offsets[None, :] < counts[:, None]
    place = jnp.where(usable, positions, -1).reshape(shards * capacity, 1)
    outgoing, moment_new = lax.cond(
        active,
        orthogonalize_kernel,
        spare_pair,
        arrived.reshape(shards * capacity, extent),
        row_index[:, None],
        momentum[0, 0],
        place,
    )
    lanes = lax.axis_size("rep")
    quarter = capacity // lanes
    returned = lax.all_to_all(outgoing, ("dp", "rep"), split_axis=0, concat_axis=0, tiled=True)
    mine = jnp.take(returned.reshape(shards * lanes, quarter, extent), owners * lanes + slot_ids, axis=0)
    picked_rows = jnp.zeros((matrices, capacity, extent), mine.dtype)
    for shift in range(lanes):
        if shift == 0:
            block = mine
        else:
            block = lax.ppermute(mine, "rep", [(q, (q + shift) % lanes) for q in range(lanes)])
        source = (rep_index - shift + lanes) % lanes
        picked_rows = lax.dynamic_update_slice(picked_rows, block, (0, source * quarter, 0))
    return (picked_rows, moment_new[None, None])


def solution(mesh):
    return jax.shard_map(
        body,
        mesh=mesh,
        in_specs=(P(None, "dp", None), P(), P(), P("dp", "rep", None, None)),
        out_specs=(P(None, "dp", None), P("dp", "rep", None, None)),
        check_vma=False,
    )
```

```python
import math

import jax
import jax.numpy as jnp
from jax import lax
from jax.experimental import pallas as pl
from jax.experimental.pallas import tpu as pltpu
from jax.sharding import PartitionSpec as P

NS_ITERS = 5


momentum_decay = 0.95
grad_share = 0.05
epsilon = 1e-06
quintic_one = 3.4445
quintic_two = -4.775
quintic_three = 2.0315


def slots_of(owners):
    total = owners.shape[0]
    same_owner = owners[:, None] == owners[None, :]
    position = jnp.arange(total, dtype=jnp.int32)
    earlier = position[None, :] < position[:, None]
    return jnp.sum((same_owner & earlier).astype(jnp.int32), axis=1)


def exclusive_starts(counts):
    shards = counts.shape[0]
    ids = jnp.arange(shards, dtype=jnp.int32)
    before = ids[None, :] < ids[:, None]
    return jnp.sum(jnp.where(before, counts[None, :], 0), axis=1)


def orthogonalize(full_grad, moment):
    extent = full_grad.shape[0]
    gradient = full_grad.astype(jnp.float32)
    moment_new = momentum_decay * moment + grad_share * gradient
    blended = grad_share * gradient + momentum_decay * moment_new
    frob_norm = jnp.sqrt(jnp.sum(blended * blended)) + epsilon
    iterate = (blended / frob_norm).astype(jnp.bfloat16)
    result = iterate
    for iteration in range(NS_ITERS):
        gram_matrix = lax.dot_general(
            iterate, iterate, (((1,), (1,)), ((), ())), preferred_element_type=jnp.float32
        ).astype(jnp.bfloat16)
        square = jnp.dot(gram_matrix, gram_matrix, preferred_element_type=jnp.float32)
        polynomial = (
            quintic_two * gram_matrix.astype(jnp.float32) + quintic_three * square
        ).astype(jnp.bfloat16)
        next_iter = quintic_one * iterate.astype(jnp.float32) + jnp.dot(
            polynomial, iterate, preferred_element_type=jnp.float32
        )
        if iteration + 1 < NS_ITERS:
            iterate = next_iter.astype(jnp.bfloat16)
        else:
            result = (math.sqrt(extent) * next_iter).astype(jnp.bfloat16)
    return (result, moment_new)


TILE = 256
TRANSPOSED = (((1,), (1,)), ((), ()))


def newton_schulz_kernel(
    slots_ref, take_ref, m_ref, place_ref, out_ref, mn_ref, g_ref, x0_ref, x1_ref, a_ref, p_ref
):
    extent = g_ref.shape[0]
    tiles = extent // TILE
    slot_total = slots_ref.shape[0]

    def rows_of(i):
        return pl.ds(pl.multiple_of(i * TILE, TILE), TILE)

    def compact_tile(i, carry):
        rows = rows_of(i)
        lanes = lax.broadcasted_iota(jnp.int32, (TILE, slot_total), 1)
        chosen = (take_ref[rows, :] == lanes).astype(jnp.bfloat16)
        g_ref[rows, :] = jnp.dot(
            chosen, slots_ref[...], preferred_element_type=jnp.float32
        ).astype(jnp.bfloat16)
        return carry

    lax.fori_loop(0, tiles, compact_tile, 0)

    def moment_tile(i, acc):
        rows = rows_of(i)
        gradient = g_ref[rows, :].astype(jnp.float32)
        moment_new = momentum_decay * m_ref[rows, :] + grad_share * gradient
        mn_ref[rows, :] = moment_new
        blended = grad_share * gradient + momentum_decay * moment_new
        return acc + jnp.sum(blended * blended, axis=0, keepdims=True)

    acc = lax.fori_loop(0, tiles, moment_tile, jnp.zeros((1, extent), jnp.float32))
    frob_norm = jnp.sqrt(jnp.sum(acc, axis=1, keepdims=True)) + epsilon

    def scale_tile(i, carry):
        rows = rows_of(i)
        gradient = g_ref[rows, :].astype(jnp.float32)
        blended = grad_share * gradient + momentum_decay * mn_ref[rows, :]
        x0_ref[rows, :] = (blended / frob_norm).astype(jnp.bfloat16)
        return carry

    lax.fori_loop(0, tiles, scale_tile, 0)
    iterates = (x0_ref, x1_ref)
    for iteration in range(NS_ITERS):
        now = iterates[iteration % 2]
        later = iterates[(iteration + 1) % 2]
        last = iteration + 1 == NS_ITERS

        def gram_tile(i, carry, now=now):
            rows = rows_of(i)
            a_ref[rows, :] = lax.dot_general(
                now[rows, :], now[...], TRANSPOSED, preferred_element_type=jnp.float32
            ).astype(jnp.bfloat16)
            return carry

        def poly_tile(i, carry):
            rows = rows_of(i)
            gram_rows = a_ref[rows, :]
            square = jnp.dot(gram_rows, a_ref[...], preferred_element_type=jnp.float32)
            p_ref[rows, :] = (
                quintic_two * gram_rows.astype(jnp.float32) + quintic_three * square
            ).astype(jnp.bfloat16)
            return carry

        def next_tile(i, carry, now=now, later=later, last=last):
            rows = rows_of(i)
            next_iter = quintic_one * now[rows, :].astype(jnp.float32) + jnp.dot(
                p_ref[rows, :], now[...], preferred_element_type=jnp.float32
            )
            if last:
                a_ref[rows, :] = (math.sqrt(extent) * next_iter).astype(jnp.bfloat16)
            else:
                later[rows, :] = next_iter.astype(jnp.bfloat16)
            return carry

        lax.fori_loop(0, tiles, gram_tile, 0)
        lax.fori_loop(0, tiles, poly_tile, 0)
        lax.fori_loop(0, tiles, next_tile, 0)

    def place_tile(i, carry):
        rows = rows_of(i)
        lanes = lax.broadcasted_iota(jnp.int32, (TILE, extent), 1)
        chosen = (place_ref[rows, :] == lanes).astype(jnp.bfloat16)
        out_ref[rows, :] = jnp.dot(
            chosen, a_ref[...], preferred_element_type=jnp.float32
        ).astype(jnp.bfloat16)
        return carry

    lax.fori_loop(0, slot_total // TILE, place_tile, 0)


def orthogonalize_kernel(slots, take, moment, place):
    extent = moment.shape[0]
    square = (extent, extent)
    vmem = pl.BlockSpec(memory_space=pltpu.VMEM)
    return pl.pallas_call(
        newton_schulz_kernel,
        out_shape=(
            jax.ShapeDtypeStruct(slots.shape, jnp.bfloat16),
            jax.ShapeDtypeStruct(square, jnp.float32),
        ),
        in_specs=[vmem, vmem, vmem, vmem],
        out_specs=(vmem, vmem),
        scratch_shapes=[pltpu.VMEM(square, jnp.bfloat16) for _ in range(5)],
        compiler_params=pltpu.CompilerParams(vmem_limit_bytes=48 * 1024 * 1024),
        cost_estimate=pl.CostEstimate(
            flops=2 * (3 * NS_ITERS + 2) * extent ** 3,
            bytes_accessed=16 * extent * extent,
            transcendentals=0,
        ),
    )(slots, take, moment, place)


def spare_pair(slots, take, moment, place):
    return (jnp.zeros(slots.shape, jnp.bfloat16), jnp.zeros(moment.shape, jnp.float32))


def body(grad_rows, row_counts, owners, momentum):
    matrices, capacity, extent = grad_rows.shape
    shards = lax.axis_size("dp")
    dp_index = lax.axis_index("dp")
    rep_index = lax.axis_index("rep")
    slot_ids = slots_of(owners)
    matrix_ids = jnp.arange(matrices, dtype=jnp.int32)
    owner_ids = jnp.arange(shards, dtype=jnp.int32)
    in_lane = slot_ids == rep_index
    lane_pick = (owners[None, :] == owner_ids[:, None]) & in_lane[None, :]
    lane_matrix = jnp.sum(jnp.where(lane_pick, matrix_ids[None, :], 0), axis=1)
    send_table = jnp.take(grad_rows, lane_matrix, axis=0, mode="clip")
    arrived = lax.all_to_all(send_table, "dp", split_axis=0, concat_axis=0, tiled=True)

    held_here = (owners == dp_index) & in_lane
    active = jnp.any(held_here)
    counts = jnp.sum(jnp.where(held_here[:, None], row_counts, 0), axis=0)
    starts = exclusive_starts(counts)
    row_ids = jnp.arange(extent, dtype=jnp.int32)
    covers = (starts[None, :] <= row_ids[:, None]) & (row_ids[:, None] < (starts + counts)[None, :])
    holder = jnp.sum(jnp.where(covers, owner_ids[None, :], 0), axis=1)
    first_row = jnp.sum(jnp.where(covers, starts[None, :], 0), axis=1)
    row_index = holder * capacity + (row_ids - first_row)
    offsets = jnp.arange(capacity, dtype=jnp.int32)
    positions = starts[:, None] + offsets[None, :]
    usable = offsets[None, :] < counts[:, None]
    place = jnp.where(usable, positions, -1).reshape(shards * capacity, 1)
    outgoing, moment_new = lax.cond(
        active,
        orthogonalize_kernel,
        spare_pair,
        arrived.reshape(shards * capacity, extent),
        row_index[:, None],
        momentum[0, 0],
        place,
    )
    lanes = lax.axis_size("rep")
    quarter = capacity // lanes
    returned = lax.all_to_all(outgoing, ("dp", "rep"), split_axis=0, concat_axis=0, tiled=True)
    mine = jnp.take(returned.reshape(shards * lanes, quarter, extent), owners * lanes + slot_ids, axis=0, mode="clip")
    def shifted(block, step):
        return lax.ppermute(block, "rep", [(q, (q + step) % lanes) for q in range(lanes)])

    half = quarter // 2
    from_left = shifted(mine, 1)
    from_right = shifted(mine, lanes - 1)
    from_far = jnp.concatenate(
        [shifted(from_left[:, :half], 1), shifted(from_right[:, half:], lanes - 1)], axis=1
    )
    picked_rows = jnp.zeros((matrices, capacity, extent), mine.dtype)
    for shift, block in ((0, mine), (1, from_left), (lanes - 1, from_right), (2, from_far)):
        source = (rep_index - shift + lanes) % lanes
        picked_rows = lax.dynamic_update_slice(picked_rows, block, (0, source * quarter, 0))
    return (picked_rows, moment_new[None, None])


def solution(mesh):
    return jax.shard_map(
        body,
        mesh=mesh,
        in_specs=(P(None, "dp", None), P(), P(), P("dp", "rep", None, None)),
        out_specs=(P(None, "dp", None), P("dp", "rep", None, None)),
        check_vma=False,
    )
```

```python
import math

import jax
import jax.numpy as jnp
from jax import lax
from jax.experimental import pallas as pl
from jax.experimental.pallas import tpu as pltpu
from jax.sharding import PartitionSpec as P

NS_ITERS = 5


momentum_decay = 0.95
grad_share = 0.05
epsilon = 1e-06
quintic_one = 3.4445
quintic_two = -4.775
quintic_three = 2.0315


def slots_of(owners):
    total = owners.shape[0]
    same_owner = owners[:, None] == owners[None, :]
    position = jnp.arange(total, dtype=jnp.int32)
    earlier = position[None, :] < position[:, None]
    return jnp.sum((same_owner & earlier).astype(jnp.int32), axis=1)


def exclusive_starts(counts):
    shards = counts.shape[0]
    ids = jnp.arange(shards, dtype=jnp.int32)
    before = ids[None, :] < ids[:, None]
    return jnp.sum(jnp.where(before, counts[None, :], 0), axis=1)


def orthogonalize(full_grad, moment):
    extent = full_grad.shape[0]
    gradient = full_grad.astype(jnp.float32)
    moment_new = momentum_decay * moment + grad_share * gradient
    blended = grad_share * gradient + momentum_decay * moment_new
    frob_norm = jnp.sqrt(jnp.sum(blended * blended)) + epsilon
    iterate = (blended / frob_norm).astype(jnp.bfloat16)
    result = iterate
    for iteration in range(NS_ITERS):
        gram_matrix = lax.dot_general(
            iterate, iterate, (((1,), (1,)), ((), ())), preferred_element_type=jnp.float32
        ).astype(jnp.bfloat16)
        square = jnp.dot(gram_matrix, gram_matrix, preferred_element_type=jnp.float32)
        polynomial = (
            quintic_two * gram_matrix.astype(jnp.float32) + quintic_three * square
        ).astype(jnp.bfloat16)
        next_iter = quintic_one * iterate.astype(jnp.float32) + jnp.dot(
            polynomial, iterate, preferred_element_type=jnp.float32
        )
        if iteration + 1 < NS_ITERS:
            iterate = next_iter.astype(jnp.bfloat16)
        else:
            result = (math.sqrt(extent) * next_iter).astype(jnp.bfloat16)
    return (result, moment_new)


TILE = 256
TRANSPOSED = (((1,), (1,)), ((), ()))


def newton_schulz_kernel(
    slots_ref, take_ref, m_ref, place_ref, out_ref, mn_ref, g_ref, x0_ref, x1_ref, a_ref, p_ref
):
    extent = g_ref.shape[0]
    tiles = extent // TILE
    slot_total = slots_ref.shape[0]

    def rows_of(i):
        return pl.ds(pl.multiple_of(i * TILE, TILE), TILE)

    def compact_tile(i, carry):
        rows = rows_of(i)
        lanes = lax.broadcasted_iota(jnp.int32, (TILE, slot_total), 1)
        chosen = (take_ref[rows, :] == lanes).astype(jnp.bfloat16)
        g_ref[rows, :] = jnp.dot(
            chosen, slots_ref[...], preferred_element_type=jnp.float32
        ).astype(jnp.bfloat16)
        return carry

    lax.fori_loop(0, tiles, compact_tile, 0)

    def moment_tile(i, acc):
        rows = rows_of(i)
        gradient = g_ref[rows, :].astype(jnp.float32)
        moment_new = momentum_decay * m_ref[rows, :] + grad_share * gradient
        mn_ref[rows, :] = moment_new
        blended = grad_share * gradient + momentum_decay * moment_new
        return acc + jnp.sum(blended * blended, axis=0, keepdims=True)

    acc = lax.fori_loop(0, tiles, moment_tile, jnp.zeros((1, extent), jnp.float32))
    frob_norm = jnp.sqrt(jnp.sum(acc, axis=1, keepdims=True)) + epsilon

    def scale_tile(i, carry):
        rows = rows_of(i)
        gradient = g_ref[rows, :].astype(jnp.float32)
        blended = grad_share * gradient + momentum_decay * mn_ref[rows, :]
        x0_ref[rows, :] = (blended / frob_norm).astype(jnp.bfloat16)
        return carry

    lax.fori_loop(0, tiles, scale_tile, 0)
    iterates = (x0_ref, x1_ref)
    for iteration in range(NS_ITERS):
        now = iterates[iteration % 2]
        later = iterates[(iteration + 1) % 2]
        last = iteration + 1 == NS_ITERS

        for i in range(tiles):
            rows = pl.ds(i * TILE, TILE)
            for j in range(i, tiles):
                cols = pl.ds(j * TILE, TILE)
                block = lax.dot_general(
                    now[rows, :], now[cols, :], TRANSPOSED, preferred_element_type=jnp.float32
                )
                a_ref[rows, cols] = block.astype(jnp.bfloat16)
                if j > i:
                    a_ref[cols, rows] = block.T.astype(jnp.bfloat16)
        for i in range(tiles):
            rows = pl.ds(i * TILE, TILE)
            for j in range(i, tiles):
                cols = pl.ds(j * TILE, TILE)
                square = jnp.dot(a_ref[rows, :], a_ref[:, cols], preferred_element_type=jnp.float32)
                block = quintic_two * a_ref[rows, cols].astype(jnp.float32) + quintic_three * square
                p_ref[rows, cols] = block.astype(jnp.bfloat16)
                if j > i:
                    p_ref[cols, rows] = block.T.astype(jnp.bfloat16)

        def next_tile(i, carry, now=now, later=later, last=last):
            rows = rows_of(i)
            next_iter = quintic_one * now[rows, :].astype(jnp.float32) + jnp.dot(
                p_ref[rows, :], now[...], preferred_element_type=jnp.float32
            )
            if last:
                a_ref[rows, :] = (math.sqrt(extent) * next_iter).astype(jnp.bfloat16)
            else:
                later[rows, :] = next_iter.astype(jnp.bfloat16)
            return carry

        lax.fori_loop(0, tiles, next_tile, 0)

    def place_tile(i, carry):
        rows = rows_of(i)
        lanes = lax.broadcasted_iota(jnp.int32, (TILE, extent), 1)
        chosen = (place_ref[rows, :] == lanes).astype(jnp.bfloat16)
        out_ref[rows, :] = jnp.dot(
            chosen, a_ref[...], preferred_element_type=jnp.float32
        ).astype(jnp.bfloat16)
        return carry

    lax.fori_loop(0, slot_total // TILE, place_tile, 0)


def orthogonalize_kernel(slots, take, moment, place):
    extent = moment.shape[0]
    square = (extent, extent)
    vmem = pl.BlockSpec(memory_space=pltpu.VMEM)
    return pl.pallas_call(
        newton_schulz_kernel,
        out_shape=(
            jax.ShapeDtypeStruct(slots.shape, jnp.bfloat16),
            jax.ShapeDtypeStruct(square, jnp.float32),
        ),
        in_specs=[vmem, vmem, vmem, vmem],
        out_specs=(vmem, vmem),
        scratch_shapes=[pltpu.VMEM(square, jnp.bfloat16) for _ in range(5)],
        compiler_params=pltpu.CompilerParams(vmem_limit_bytes=48 * 1024 * 1024),
        cost_estimate=pl.CostEstimate(
            flops=2 * (3 * NS_ITERS + 2) * extent ** 3,
            bytes_accessed=16 * extent * extent,
            transcendentals=0,
        ),
    )(slots, take, moment, place)


def spare_pair(slots, take, moment, place):
    return (jnp.zeros(slots.shape, jnp.bfloat16), jnp.zeros(moment.shape, jnp.float32))


def body(grad_rows, row_counts, owners, momentum):
    matrices, capacity, extent = grad_rows.shape
    shards = lax.axis_size("dp")
    dp_index = lax.axis_index("dp")
    rep_index = lax.axis_index("rep")
    slot_ids = slots_of(owners)
    matrix_ids = jnp.arange(matrices, dtype=jnp.int32)
    owner_ids = jnp.arange(shards, dtype=jnp.int32)
    in_lane = slot_ids == rep_index
    lane_pick = (owners[None, :] == owner_ids[:, None]) & in_lane[None, :]
    lane_matrix = jnp.sum(jnp.where(lane_pick, matrix_ids[None, :], 0), axis=1)
    send_table = jnp.take(grad_rows, lane_matrix, axis=0, mode="clip")
    arrived = lax.all_to_all(send_table, "dp", split_axis=0, concat_axis=0, tiled=True)

    held_here = (owners == dp_index) & in_lane
    active = jnp.any(held_here)
    counts = jnp.sum(jnp.where(held_here[:, None], row_counts, 0), axis=0)
    starts = exclusive_starts(counts)
    row_ids = jnp.arange(extent, dtype=jnp.int32)
    covers = (starts[None, :] <= row_ids[:, None]) & (row_ids[:, None] < (starts + counts)[None, :])
    holder = jnp.sum(jnp.where(covers, owner_ids[None, :], 0), axis=1)
    first_row = jnp.sum(jnp.where(covers, starts[None, :], 0), axis=1)
    row_index = holder * capacity + (row_ids - first_row)
    offsets = jnp.arange(capacity, dtype=jnp.int32)
    positions = starts[:, None] + offsets[None, :]
    usable = offsets[None, :] < counts[:, None]
    place = jnp.where(usable, positions, -1).reshape(shards * capacity, 1)
    outgoing, moment_new = lax.cond(
        active,
        orthogonalize_kernel,
        spare_pair,
        arrived.reshape(shards * capacity, extent),
        row_index[:, None],
        momentum[0, 0],
        place,
    )
    lanes = lax.axis_size("rep")
    quarter = capacity // lanes
    returned = lax.all_to_all(outgoing, ("dp", "rep"), split_axis=0, concat_axis=0, tiled=True)
    mine = jnp.take(returned.reshape(shards * lanes, quarter, extent), owners * lanes + slot_ids, axis=0, mode="clip")
    def shifted(block, step):
        return lax.ppermute(block, "rep", [(q, (q + step) % lanes) for q in range(lanes)])

    half = quarter // 2
    from_left = shifted(mine, 1)
    from_right = shifted(mine, lanes - 1)
    from_far = jnp.concatenate(
        [shifted(from_left[:, :half], 1), shifted(from_right[:, half:], lanes - 1)], axis=1
    )
    picked_rows = jnp.zeros((matrices, capacity, extent), mine.dtype)
    for shift, block in ((0, mine), (1, from_left), (lanes - 1, from_right), (2, from_far)):
        source = (rep_index - shift + lanes) % lanes
        picked_rows = lax.dynamic_update_slice(picked_rows, block, (0, source * quarter, 0))
    return (picked_rows, moment_new[None, None])


def solution(mesh):
    return jax.shard_map(
        body,
        mesh=mesh,
        in_specs=(P(None, "dp", None), P(), P(), P("dp", "rep", None, None)),
        out_specs=(P(None, "dp", None), P("dp", "rep", None, None)),
        check_vma=False,
    )
```

```python
import math

import jax
import jax.numpy as jnp
from jax import lax
from jax.experimental import pallas as pl
from jax.experimental.pallas import tpu as pltpu
from jax.sharding import PartitionSpec as P

NS_ITERS = 5


momentum_decay = 0.95
grad_share = 0.05
epsilon = 1e-06
quintic_one = 3.4445
quintic_two = -4.775
quintic_three = 2.0315


def slots_of(owners):
    total = owners.shape[0]
    same_owner = owners[:, None] == owners[None, :]
    position = jnp.arange(total, dtype=jnp.int32)
    earlier = position[None, :] < position[:, None]
    return jnp.sum((same_owner & earlier).astype(jnp.int32), axis=1)


def exclusive_starts(counts):
    shards = counts.shape[0]
    ids = jnp.arange(shards, dtype=jnp.int32)
    before = ids[None, :] < ids[:, None]
    return jnp.sum(jnp.where(before, counts[None, :], 0), axis=1)


def orthogonalize(full_grad, moment):
    extent = full_grad.shape[0]
    gradient = full_grad.astype(jnp.float32)
    moment_new = momentum_decay * moment + grad_share * gradient
    blended = grad_share * gradient + momentum_decay * moment_new
    frob_norm = jnp.sqrt(jnp.sum(blended * blended)) + epsilon
    iterate = (blended / frob_norm).astype(jnp.bfloat16)
    result = iterate
    for iteration in range(NS_ITERS):
        gram_matrix = lax.dot_general(
            iterate, iterate, (((1,), (1,)), ((), ())), preferred_element_type=jnp.float32
        ).astype(jnp.bfloat16)
        square = jnp.dot(gram_matrix, gram_matrix, preferred_element_type=jnp.float32)
        polynomial = (
            quintic_two * gram_matrix.astype(jnp.float32) + quintic_three * square
        ).astype(jnp.bfloat16)
        next_iter = quintic_one * iterate.astype(jnp.float32) + jnp.dot(
            polynomial, iterate, preferred_element_type=jnp.float32
        )
        if iteration + 1 < NS_ITERS:
            iterate = next_iter.astype(jnp.bfloat16)
        else:
            result = (math.sqrt(extent) * next_iter).astype(jnp.bfloat16)
    return (result, moment_new)


TILE = 256
TRANSPOSED = (((1,), (1,)), ((), ()))


def newton_schulz_kernel(
    slots_ref, take_ref, m_ref, place_ref, out_ref, mn_ref, g_ref, x0_ref, x1_ref, a_ref, p_ref
):
    extent = g_ref.shape[0]
    tiles = extent // TILE
    slot_total = slots_ref.shape[0]

    def rows_of(i):
        return pl.ds(pl.multiple_of(i * TILE, TILE), TILE)

    for i in range(tiles):
        rows = pl.ds(i * TILE, TILE)
        lanes = i * TILE + lax.broadcasted_iota(jnp.int32, (TILE, slot_total - i * TILE), 1)
        chosen = (take_ref[rows, :] == lanes).astype(jnp.bfloat16)
        g_ref[rows, :] = jnp.dot(
            chosen, slots_ref[i * TILE :, :], preferred_element_type=jnp.float32
        ).astype(jnp.bfloat16)

    def moment_tile(i, acc):
        rows = rows_of(i)
        gradient = g_ref[rows, :].astype(jnp.float32)
        moment_new = momentum_decay * m_ref[rows, :] + grad_share * gradient
        mn_ref[rows, :] = moment_new
        blended = grad_share * gradient + momentum_decay * moment_new
        return acc + jnp.sum(blended * blended, axis=0, keepdims=True)

    acc = lax.fori_loop(0, tiles, moment_tile, jnp.zeros((1, extent), jnp.float32))
    frob_norm = jnp.sqrt(jnp.sum(acc, axis=1, keepdims=True)) + epsilon

    def scale_tile(i, carry):
        rows = rows_of(i)
        gradient = g_ref[rows, :].astype(jnp.float32)
        blended = grad_share * gradient + momentum_decay * mn_ref[rows, :]
        x0_ref[rows, :] = (blended / frob_norm).astype(jnp.bfloat16)
        return carry

    lax.fori_loop(0, tiles, scale_tile, 0)
    iterates = (x0_ref, x1_ref)
    for iteration in range(NS_ITERS):
        now = iterates[iteration % 2]
        later = iterates[(iteration + 1) % 2]
        last = iteration + 1 == NS_ITERS

        for i in range(tiles):
            rows = pl.ds(i * TILE, TILE)
            for j in range(i, tiles):
                cols = pl.ds(j * TILE, TILE)
                block = lax.dot_general(
                    now[rows, :], now[cols, :], TRANSPOSED, preferred_element_type=jnp.float32
                )
                a_ref[rows, cols] = block.astype(jnp.bfloat16)
                if j > i:
                    a_ref[cols, rows] = block.T.astype(jnp.bfloat16)
        for i in range(tiles):
            rows = pl.ds(i * TILE, TILE)
            for j in range(i, tiles):
                cols = pl.ds(j * TILE, TILE)
                square = jnp.dot(a_ref[rows, :], a_ref[:, cols], preferred_element_type=jnp.float32)
                block = quintic_two * a_ref[rows, cols].astype(jnp.float32) + quintic_three * square
                p_ref[rows, cols] = block.astype(jnp.bfloat16)
                if j > i:
                    p_ref[cols, rows] = block.T.astype(jnp.bfloat16)

        def next_tile(i, carry, now=now, later=later, last=last):
            rows = rows_of(i)
            next_iter = quintic_one * now[rows, :].astype(jnp.float32) + jnp.dot(
                p_ref[rows, :], now[...], preferred_element_type=jnp.float32
            )
            if last:
                a_ref[rows, :] = (math.sqrt(extent) * next_iter).astype(jnp.bfloat16)
            else:
                later[rows, :] = next_iter.astype(jnp.bfloat16)
            return carry

        lax.fori_loop(0, tiles, next_tile, 0)

    for i in range(slot_total // TILE):
        rows = pl.ds(i * TILE, TILE)
        reach = min(extent, (i + 1) * TILE)
        lanes = lax.broadcasted_iota(jnp.int32, (TILE, reach), 1)
        chosen = (place_ref[rows, :] == lanes).astype(jnp.bfloat16)
        out_ref[rows, :] = jnp.dot(
            chosen, a_ref[:reach, :], preferred_element_type=jnp.float32
        ).astype(jnp.bfloat16)


def orthogonalize_kernel(slots, take, moment, place):
    extent = moment.shape[0]
    square = (extent, extent)
    vmem = pl.BlockSpec(memory_space=pltpu.VMEM)
    return pl.pallas_call(
        newton_schulz_kernel,
        out_shape=(
            jax.ShapeDtypeStruct(slots.shape, jnp.bfloat16),
            jax.ShapeDtypeStruct(square, jnp.float32),
        ),
        in_specs=[vmem, vmem, vmem, vmem],
        out_specs=(vmem, vmem),
        scratch_shapes=[pltpu.VMEM(square, jnp.bfloat16) for _ in range(5)],
        compiler_params=pltpu.CompilerParams(vmem_limit_bytes=48 * 1024 * 1024),
        cost_estimate=pl.CostEstimate(
            flops=2 * (3 * NS_ITERS + 2) * extent ** 3,
            bytes_accessed=16 * extent * extent,
            transcendentals=0,
        ),
    )(slots, take, moment, place)


def spare_pair(slots, take, moment, place):
    return (jnp.zeros(slots.shape, jnp.bfloat16), jnp.zeros(moment.shape, jnp.float32))


def body(grad_rows, row_counts, owners, momentum):
    matrices, capacity, extent = grad_rows.shape
    shards = lax.axis_size("dp")
    dp_index = lax.axis_index("dp")
    rep_index = lax.axis_index("rep")
    slot_ids = slots_of(owners)
    matrix_ids = jnp.arange(matrices, dtype=jnp.int32)
    owner_ids = jnp.arange(shards, dtype=jnp.int32)
    in_lane = slot_ids == rep_index
    lane_pick = (owners[None, :] == owner_ids[:, None]) & in_lane[None, :]
    lane_matrix = jnp.sum(jnp.where(lane_pick, matrix_ids[None, :], 0), axis=1)
    send_table = jnp.take(grad_rows, lane_matrix, axis=0, mode="clip")
    arrived = lax.all_to_all(send_table, "dp", split_axis=0, concat_axis=0, tiled=True)

    held_here = (owners == dp_index) & in_lane
    active = jnp.any(held_here)
    counts = jnp.sum(jnp.where(held_here[:, None], row_counts, 0), axis=0)
    starts = exclusive_starts(counts)
    row_ids = jnp.arange(extent, dtype=jnp.int32)
    covers = (starts[None, :] <= row_ids[:, None]) & (row_ids[:, None] < (starts + counts)[None, :])
    holder = jnp.sum(jnp.where(covers, owner_ids[None, :], 0), axis=1)
    first_row = jnp.sum(jnp.where(covers, starts[None, :], 0), axis=1)
    row_index = holder * capacity + (row_ids - first_row)
    offsets = jnp.arange(capacity, dtype=jnp.int32)
    positions = starts[:, None] + offsets[None, :]
    usable = offsets[None, :] < counts[:, None]
    place = jnp.where(usable, positions, -1).reshape(shards * capacity, 1)
    outgoing, moment_new = lax.cond(
        active,
        orthogonalize_kernel,
        spare_pair,
        arrived.reshape(shards * capacity, extent),
        row_index[:, None],
        momentum[0, 0],
        place,
    )
    lanes = lax.axis_size("rep")
    quarter = capacity // lanes
    returned = lax.all_to_all(outgoing, ("dp", "rep"), split_axis=0, concat_axis=0, tiled=True)
    mine = jnp.take(returned.reshape(shards * lanes, quarter, extent), owners * lanes + slot_ids, axis=0, mode="clip")
    def shifted(block, step):
        return lax.ppermute(block, "rep", [(q, (q + step) % lanes) for q in range(lanes)])

    half = quarter // 2
    from_left = shifted(mine, 1)
    from_right = shifted(mine, lanes - 1)
    from_far = jnp.concatenate(
        [shifted(from_left[:, :half], 1), shifted(from_right[:, half:], lanes - 1)], axis=1
    )
    picked_rows = jnp.zeros((matrices, capacity, extent), mine.dtype)
    for shift, block in ((0, mine), (1, from_left), (lanes - 1, from_right), (2, from_far)):
        source = (rep_index - shift + lanes) % lanes
        picked_rows = lax.dynamic_update_slice(picked_rows, block, (0, source * quarter, 0))
    return (picked_rows, moment_new[None, None])


def solution(mesh):
    return jax.shard_map(
        body,
        mesh=mesh,
        in_specs=(P(None, "dp", None), P(), P(), P("dp", "rep", None, None)),
        out_specs=(P(None, "dp", None), P("dp", "rep", None, None)),
        check_vma=False,
    )
```

```python
import math

import jax
import jax.numpy as jnp
from jax import lax
from jax.experimental import pallas as pl
from jax.experimental.pallas import tpu as pltpu
from jax.sharding import PartitionSpec as P

NS_ITERS = 5


momentum_decay = 0.95
grad_share = 0.05
epsilon = 1e-06
quintic_one = 3.4445
quintic_two = -4.775
quintic_three = 2.0315


def slots_of(owners):
    total = owners.shape[0]
    same_owner = owners[:, None] == owners[None, :]
    position = jnp.arange(total, dtype=jnp.int32)
    earlier = position[None, :] < position[:, None]
    return jnp.sum((same_owner & earlier).astype(jnp.int32), axis=1)


def exclusive_starts(counts):
    shards = counts.shape[0]
    ids = jnp.arange(shards, dtype=jnp.int32)
    before = ids[None, :] < ids[:, None]
    return jnp.sum(jnp.where(before, counts[None, :], 0), axis=1)


def orthogonalize(full_grad, moment):
    extent = full_grad.shape[0]
    gradient = full_grad.astype(jnp.float32)
    moment_new = momentum_decay * moment + grad_share * gradient
    blended = grad_share * gradient + momentum_decay * moment_new
    frob_norm = jnp.sqrt(jnp.sum(blended * blended)) + epsilon
    iterate = (blended / frob_norm).astype(jnp.bfloat16)
    result = iterate
    for iteration in range(NS_ITERS):
        gram_matrix = lax.dot_general(
            iterate, iterate, (((1,), (1,)), ((), ())), preferred_element_type=jnp.float32
        ).astype(jnp.bfloat16)
        square = jnp.dot(gram_matrix, gram_matrix, preferred_element_type=jnp.float32)
        polynomial = (
            quintic_two * gram_matrix.astype(jnp.float32) + quintic_three * square
        ).astype(jnp.bfloat16)
        next_iter = quintic_one * iterate.astype(jnp.float32) + jnp.dot(
            polynomial, iterate, preferred_element_type=jnp.float32
        )
        if iteration + 1 < NS_ITERS:
            iterate = next_iter.astype(jnp.bfloat16)
        else:
            result = (math.sqrt(extent) * next_iter).astype(jnp.bfloat16)
    return (result, moment_new)


TILE = 256
TRANSPOSED = (((1,), (1,)), ((), ()))


def newton_schulz_kernel(
    slots_ref, take_ref, m_ref, place_ref, out_ref, mn_ref, g_ref, x0_ref, x1_ref, a_ref, p_ref
):
    extent = g_ref.shape[0]
    tiles = extent // TILE
    slot_total = slots_ref.shape[0]

    def rows_of(i):
        return pl.ds(i * TILE, TILE)

    for i in range(tiles):
        rows = pl.ds(i * TILE, TILE)
        lanes = i * TILE + lax.broadcasted_iota(jnp.int32, (TILE, slot_total - i * TILE), 1)
        chosen = (take_ref[rows, :] == lanes).astype(jnp.bfloat16)
        g_ref[rows, :] = jnp.dot(
            chosen, slots_ref[i * TILE :, :], preferred_element_type=jnp.float32
        ).astype(jnp.bfloat16)

    def moment_tile(i, acc):
        rows = rows_of(i)
        gradient = g_ref[rows, :].astype(jnp.float32)
        moment_new = momentum_decay * m_ref[rows, :] + grad_share * gradient
        mn_ref[rows, :] = moment_new
        blended = grad_share * gradient + momentum_decay * moment_new
        return acc + jnp.sum(blended * blended, axis=0, keepdims=True)

    acc = jnp.zeros((1, extent), jnp.float32)
    for i in range(tiles):
        acc = moment_tile(i, acc)
    frob_norm = jnp.sqrt(jnp.sum(acc, axis=1, keepdims=True)) + epsilon

    def scale_tile(i, carry):
        rows = rows_of(i)
        gradient = g_ref[rows, :].astype(jnp.float32)
        blended = grad_share * gradient + momentum_decay * mn_ref[rows, :]
        x0_ref[rows, :] = (blended / frob_norm).astype(jnp.bfloat16)
        return carry

    for i in range(tiles):
        scale_tile(i, 0)
    iterates = (x0_ref, x1_ref)
    for iteration in range(NS_ITERS):
        now = iterates[iteration % 2]
        later = iterates[(iteration + 1) % 2]
        last = iteration + 1 == NS_ITERS

        for i in range(tiles):
            rows = pl.ds(i * TILE, TILE)
            for j in range(i, tiles):
                cols = pl.ds(j * TILE, TILE)
                block = lax.dot_general(
                    now[rows, :], now[cols, :], TRANSPOSED, preferred_element_type=jnp.float32
                )
                a_ref[rows, cols] = block.astype(jnp.bfloat16)
                if j > i:
                    a_ref[cols, rows] = block.T.astype(jnp.bfloat16)
        for i in range(tiles):
            rows = pl.ds(i * TILE, TILE)
            for j in range(i, tiles):
                cols = pl.ds(j * TILE, TILE)
                square = jnp.dot(a_ref[rows, :], a_ref[:, cols], preferred_element_type=jnp.float32)
                block = quintic_two * a_ref[rows, cols].astype(jnp.float32) + quintic_three * square
                p_ref[rows, cols] = block.astype(jnp.bfloat16)
                if j > i:
                    p_ref[cols, rows] = block.T.astype(jnp.bfloat16)

        def next_tile(i, carry, now=now, later=later, last=last):
            rows = rows_of(i)
            next_iter = quintic_one * now[rows, :].astype(jnp.float32) + jnp.dot(
                p_ref[rows, :], now[...], preferred_element_type=jnp.float32
            )
            if last:
                a_ref[rows, :] = (math.sqrt(extent) * next_iter).astype(jnp.bfloat16)
            else:
                later[rows, :] = next_iter.astype(jnp.bfloat16)
            return carry

        for i in range(tiles):
            next_tile(i, 0)

    for i in range(slot_total // TILE):
        rows = pl.ds(i * TILE, TILE)
        reach = min(extent, (i + 1) * TILE)
        lanes = lax.broadcasted_iota(jnp.int32, (TILE, reach), 1)
        chosen = (place_ref[rows, :] == lanes).astype(jnp.bfloat16)
        out_ref[rows, :] = jnp.dot(
            chosen, a_ref[:reach, :], preferred_element_type=jnp.float32
        ).astype(jnp.bfloat16)


def orthogonalize_kernel(slots, take, moment, place):
    extent = moment.shape[0]
    square = (extent, extent)
    vmem = pl.BlockSpec(memory_space=pltpu.VMEM)
    return pl.pallas_call(
        newton_schulz_kernel,
        out_shape=(
            jax.ShapeDtypeStruct(slots.shape, jnp.bfloat16),
            jax.ShapeDtypeStruct(square, jnp.float32),
        ),
        in_specs=[vmem, vmem, vmem, vmem],
        out_specs=(vmem, vmem),
        scratch_shapes=[pltpu.VMEM(square, jnp.bfloat16) for _ in range(5)],
        compiler_params=pltpu.CompilerParams(vmem_limit_bytes=48 * 1024 * 1024),
        cost_estimate=pl.CostEstimate(
            flops=2 * (3 * NS_ITERS + 2) * extent ** 3,
            bytes_accessed=16 * extent * extent,
            transcendentals=0,
        ),
    )(slots, take, moment, place)


def spare_pair(slots, take, moment, place):
    return (jnp.zeros(slots.shape, jnp.bfloat16), jnp.zeros(moment.shape, jnp.float32))


def body(grad_rows, row_counts, owners, momentum):
    matrices, capacity, extent = grad_rows.shape
    shards = lax.axis_size("dp")
    dp_index = lax.axis_index("dp")
    rep_index = lax.axis_index("rep")
    slot_ids = slots_of(owners)
    matrix_ids = jnp.arange(matrices, dtype=jnp.int32)
    owner_ids = jnp.arange(shards, dtype=jnp.int32)
    in_lane = slot_ids == rep_index
    lane_pick = (owners[None, :] == owner_ids[:, None]) & in_lane[None, :]
    lane_matrix = jnp.sum(jnp.where(lane_pick, matrix_ids[None, :], 0), axis=1)
    send_table = jnp.take(grad_rows, lane_matrix, axis=0, mode="clip")
    arrived = lax.all_to_all(send_table, "dp", split_axis=0, concat_axis=0, tiled=True)

    held_here = (owners == dp_index) & in_lane
    active = jnp.any(held_here)
    counts = jnp.sum(jnp.where(held_here[:, None], row_counts, 0), axis=0)
    starts = exclusive_starts(counts)
    row_ids = jnp.arange(extent, dtype=jnp.int32)
    covers = (starts[None, :] <= row_ids[:, None]) & (row_ids[:, None] < (starts + counts)[None, :])
    holder = jnp.sum(jnp.where(covers, owner_ids[None, :], 0), axis=1)
    first_row = jnp.sum(jnp.where(covers, starts[None, :], 0), axis=1)
    row_index = holder * capacity + (row_ids - first_row)
    offsets = jnp.arange(capacity, dtype=jnp.int32)
    positions = starts[:, None] + offsets[None, :]
    usable = offsets[None, :] < counts[:, None]
    place = jnp.where(usable, positions, -1).reshape(shards * capacity, 1)
    outgoing, moment_new = lax.cond(
        active,
        orthogonalize_kernel,
        spare_pair,
        arrived.reshape(shards * capacity, extent),
        row_index[:, None],
        momentum[0, 0],
        place,
    )
    lanes = lax.axis_size("rep")
    quarter = capacity // lanes
    returned = lax.all_to_all(outgoing, ("dp", "rep"), split_axis=0, concat_axis=0, tiled=True)
    mine = jnp.take(returned.reshape(shards * lanes, quarter, extent), owners * lanes + slot_ids, axis=0, mode="clip")
    def shifted(block, step):
        return lax.ppermute(block, "rep", [(q, (q + step) % lanes) for q in range(lanes)])

    half = quarter // 2
    from_left = shifted(mine, 1)
    from_right = shifted(mine, lanes - 1)
    from_far = jnp.concatenate(
        [shifted(from_left[:, :half], 1), shifted(from_right[:, half:], lanes - 1)], axis=1
    )
    picked_rows = jnp.zeros((matrices, capacity, extent), mine.dtype)
    for shift, block in ((0, mine), (1, from_left), (lanes - 1, from_right), (2, from_far)):
        source = (rep_index - shift + lanes) % lanes
        picked_rows = lax.dynamic_update_slice(picked_rows, block, (0, source * quarter, 0))
    return (picked_rows, moment_new[None, None])


def solution(mesh):
    return jax.shard_map(
        body,
        mesh=mesh,
        in_specs=(P(None, "dp", None), P(), P(), P("dp", "rep", None, None)),
        out_specs=(P(None, "dp", None), P("dp", "rep", None, None)),
        check_vma=False,
    )
```

```python
import math

import jax
import jax.numpy as jnp
from jax import lax
from jax.experimental import pallas as pl
from jax.experimental.pallas import tpu as pltpu
from jax.sharding import PartitionSpec as P

NS_ITERS = 5


momentum_decay = 0.95
grad_share = 0.05
epsilon = 1e-06
quintic_one = 3.4445
quintic_two = -4.775
quintic_three = 2.0315


def slots_of(owners):
    total = owners.shape[0]
    same_owner = owners[:, None] == owners[None, :]
    position = jnp.arange(total, dtype=jnp.int32)
    earlier = position[None, :] < position[:, None]
    return jnp.sum((same_owner & earlier).astype(jnp.int32), axis=1)


def exclusive_starts(counts):
    shards = counts.shape[0]
    ids = jnp.arange(shards, dtype=jnp.int32)
    before = ids[None, :] < ids[:, None]
    return jnp.sum(jnp.where(before, counts[None, :], 0), axis=1)


def orthogonalize(full_grad, moment):
    extent = full_grad.shape[0]
    gradient = full_grad.astype(jnp.float32)
    moment_new = momentum_decay * moment + grad_share * gradient
    blended = grad_share * gradient + momentum_decay * moment_new
    frob_norm = jnp.sqrt(jnp.sum(blended * blended)) + epsilon
    iterate = (blended / frob_norm).astype(jnp.bfloat16)
    result = iterate
    for iteration in range(NS_ITERS):
        gram_matrix = lax.dot_general(
            iterate, iterate, (((1,), (1,)), ((), ())), preferred_element_type=jnp.float32
        ).astype(jnp.bfloat16)
        square = jnp.dot(gram_matrix, gram_matrix, preferred_element_type=jnp.float32)
        polynomial = (
            quintic_two * gram_matrix.astype(jnp.float32) + quintic_three * square
        ).astype(jnp.bfloat16)
        next_iter = quintic_one * iterate.astype(jnp.float32) + jnp.dot(
            polynomial, iterate, preferred_element_type=jnp.float32
        )
        if iteration + 1 < NS_ITERS:
            iterate = next_iter.astype(jnp.bfloat16)
        else:
            result = (math.sqrt(extent) * next_iter).astype(jnp.bfloat16)
    return (result, moment_new)


TILE = 256
TRANSPOSED = (((1,), (1,)), ((), ()))


def newton_schulz_kernel(
    slots_ref, take_ref, m_ref, place_ref, out_ref, mn_ref, g_ref, x0_ref, x1_ref, a_ref, p_ref
):
    extent = g_ref.shape[0]
    tiles = extent // TILE
    slot_total = slots_ref.shape[0]

    def rows_of(i):
        return pl.ds(i * TILE, TILE)

    for i in range(tiles):
        rows = pl.ds(i * TILE, TILE)
        lanes = i * TILE + lax.broadcasted_iota(jnp.int32, (TILE, slot_total - i * TILE), 1)
        chosen = (take_ref[rows, :] == lanes).astype(jnp.bfloat16)
        g_ref[rows, :] = jnp.dot(
            chosen, slots_ref[i * TILE :, :], preferred_element_type=jnp.float32
        ).astype(jnp.bfloat16)

    def moment_tile(i, acc):
        rows = rows_of(i)
        gradient = g_ref[rows, :].astype(jnp.float32)
        moment_new = momentum_decay * m_ref[rows, :] + grad_share * gradient
        mn_ref[rows, :] = moment_new
        blended = grad_share * gradient + momentum_decay * moment_new
        return acc + jnp.sum(blended * blended, axis=0, keepdims=True)

    acc = jnp.zeros((1, extent), jnp.float32)
    for i in range(tiles):
        acc = moment_tile(i, acc)
    frob_norm = jnp.sqrt(jnp.sum(acc, axis=1, keepdims=True)) + epsilon

    def scale_tile(i, carry):
        rows = rows_of(i)
        gradient = g_ref[rows, :].astype(jnp.float32)
        blended = grad_share * gradient + momentum_decay * mn_ref[rows, :]
        x0_ref[rows, :] = (blended / frob_norm).astype(jnp.bfloat16)
        return carry

    for i in range(tiles):
        scale_tile(i, 0)
    iterates = (x0_ref, x1_ref)
    for iteration in range(NS_ITERS):
        now = iterates[iteration % 2]
        later = iterates[(iteration + 1) % 2]
        last = iteration + 1 == NS_ITERS

        for i in range(tiles):
            rows = pl.ds(i * TILE, TILE)
            for j in range(i, tiles):
                cols = pl.ds(j * TILE, TILE)
                block = lax.dot_general(
                    now[rows, :], now[cols, :], TRANSPOSED, preferred_element_type=jnp.float32
                )
                a_ref[rows, cols] = block.astype(jnp.bfloat16)
                if j > i:
                    a_ref[cols, rows] = block.T.astype(jnp.bfloat16)
        for i in range(tiles):
            rows = pl.ds(i * TILE, TILE)
            for j in range(i, tiles):
                cols = pl.ds(j * TILE, TILE)
                square = jnp.dot(a_ref[rows, :], a_ref[:, cols], preferred_element_type=jnp.float32)
                block = quintic_two * a_ref[rows, cols].astype(jnp.float32) + quintic_three * square
                p_ref[rows, cols] = block.astype(jnp.bfloat16)
                if j > i:
                    p_ref[cols, rows] = block.T.astype(jnp.bfloat16)

        def next_tile(i, carry, now=now, later=later, last=last):
            rows = rows_of(i)
            next_iter = quintic_one * now[rows, :].astype(jnp.float32) + jnp.dot(
                p_ref[rows, :], now[...], preferred_element_type=jnp.float32
            )
            if last:
                a_ref[rows, :] = (math.sqrt(extent) * next_iter).astype(jnp.bfloat16)
            else:
                later[rows, :] = next_iter.astype(jnp.bfloat16)
            return carry

        for i in range(tiles):
            next_tile(i, 0)

    for i in range(slot_total // TILE):
        rows = pl.ds(i * TILE, TILE)
        reach = min(extent, (i + 1) * TILE)
        lanes = lax.broadcasted_iota(jnp.int32, (TILE, reach), 1)
        chosen = (place_ref[rows, :] == lanes).astype(jnp.bfloat16)
        out_ref[rows, :] = jnp.dot(
            chosen, a_ref[:reach, :], preferred_element_type=jnp.float32
        ).astype(jnp.bfloat16)


def orthogonalize_kernel(slots, take, moment, place):
    extent = moment.shape[0]
    square = (extent, extent)
    vmem = pl.BlockSpec(memory_space=pltpu.VMEM)
    return pl.pallas_call(
        newton_schulz_kernel,
        out_shape=(
            jax.ShapeDtypeStruct(slots.shape, jnp.bfloat16),
            jax.ShapeDtypeStruct(square, jnp.float32),
        ),
        in_specs=[vmem, vmem, vmem, vmem],
        out_specs=(vmem, vmem),
        scratch_shapes=[pltpu.VMEM(square, jnp.bfloat16) for _ in range(5)],
        compiler_params=pltpu.CompilerParams(vmem_limit_bytes=48 * 1024 * 1024),
        cost_estimate=pl.CostEstimate(
            flops=2 * (3 * NS_ITERS + 2) * extent ** 3,
            bytes_accessed=16 * extent * extent,
            transcendentals=0,
        ),
    )(slots, take, moment, place)


def spare_pair(slots, take, moment, place):
    return (jnp.zeros(slots.shape, jnp.bfloat16), jnp.zeros(moment.shape, jnp.float32))


def body(grad_rows, row_counts, owners, momentum):
    matrices, capacity, extent = grad_rows.shape
    shards = lax.axis_size("dp")
    dp_index = lax.axis_index("dp")
    rep_index = lax.axis_index("rep")
    slot_ids = slots_of(owners)
    matrix_ids = jnp.arange(matrices, dtype=jnp.int32)
    owner_ids = jnp.arange(shards, dtype=jnp.int32)
    in_lane = slot_ids == rep_index
    lane_pick = (owners[None, :] == owner_ids[:, None]) & in_lane[None, :]
    lane_matrix = jnp.sum(jnp.where(lane_pick, matrix_ids[None, :], 0), axis=1)
    send_table = jnp.take(grad_rows, lane_matrix, axis=0, mode="clip")
    arrived = lax.all_to_all(send_table, "dp", split_axis=0, concat_axis=0, tiled=True)

    held_here = (owners == dp_index) & in_lane
    active = jnp.any(held_here)
    counts = jnp.sum(jnp.where(held_here[:, None], row_counts, 0), axis=0)
    starts = exclusive_starts(counts)
    row_ids = jnp.arange(extent, dtype=jnp.int32)
    covers = (starts[None, :] <= row_ids[:, None]) & (row_ids[:, None] < (starts + counts)[None, :])
    holder = jnp.sum(jnp.where(covers, owner_ids[None, :], 0), axis=1)
    first_row = jnp.sum(jnp.where(covers, starts[None, :], 0), axis=1)
    row_index = holder * capacity + (row_ids - first_row)
    offsets = jnp.arange(capacity, dtype=jnp.int32)
    positions = starts[:, None] + offsets[None, :]
    usable = offsets[None, :] < counts[:, None]
    place = jnp.where(usable, positions, -1).reshape(shards * capacity, 1)
    take, place, active = lax.optimization_barrier((row_index[:, None], place, active))
    outgoing, moment_new = lax.cond(
        active,
        orthogonalize_kernel,
        spare_pair,
        arrived.reshape(shards * capacity, extent),
        take,
        momentum[0, 0],
        place,
    )
    lanes = lax.axis_size("rep")
    quarter = capacity // lanes
    returned = lax.all_to_all(outgoing, ("dp", "rep"), split_axis=0, concat_axis=0, tiled=True)
    mine = jnp.take(returned.reshape(shards * lanes, quarter, extent), owners * lanes + slot_ids, axis=0, mode="clip")
    def shifted(block, step):
        return lax.ppermute(block, "rep", [(q, (q + step) % lanes) for q in range(lanes)])

    half = quarter // 2
    from_left = shifted(mine, 1)
    from_right = shifted(mine, lanes - 1)
    from_far = jnp.concatenate(
        [shifted(from_left[:, :half], 1), shifted(from_right[:, half:], lanes - 1)], axis=1
    )
    picked_rows = jnp.zeros((matrices, capacity, extent), mine.dtype)
    for shift, block in ((0, mine), (1, from_left), (lanes - 1, from_right), (2, from_far)):
        source = (rep_index - shift + lanes) % lanes
        picked_rows = lax.dynamic_update_slice(picked_rows, block, (0, source * quarter, 0))
    return (picked_rows, moment_new[None, None])


def solution(mesh):
    return jax.shard_map(
        body,
        mesh=mesh,
        in_specs=(P(None, "dp", None), P(), P(), P("dp", "rep", None, None)),
        out_specs=(P(None, "dp", None), P("dp", "rep", None, None)),
        check_vma=False,
    )
```

```python
import math

import jax
import jax.numpy as jnp
from jax import lax
from jax.experimental import pallas as pl
from jax.experimental.pallas import tpu as pltpu
from jax.sharding import PartitionSpec as P

NS_ITERS = 5


momentum_decay = 0.95
grad_share = 0.05
epsilon = 1e-06
quintic_one = 3.4445
quintic_two = -4.775
quintic_three = 2.0315


def slots_of(owners):
    total = owners.shape[0]
    same_owner = owners[:, None] == owners[None, :]
    position = jnp.arange(total, dtype=jnp.int32)
    earlier = position[None, :] < position[:, None]
    return jnp.sum((same_owner & earlier).astype(jnp.int32), axis=1)


def exclusive_starts(counts):
    shards = counts.shape[0]
    ids = jnp.arange(shards, dtype=jnp.int32)
    before = ids[None, :] < ids[:, None]
    return jnp.sum(jnp.where(before, counts[None, :], 0), axis=1)


def orthogonalize(full_grad, moment):
    extent = full_grad.shape[0]
    gradient = full_grad.astype(jnp.float32)
    moment_new = momentum_decay * moment + grad_share * gradient
    blended = grad_share * gradient + momentum_decay * moment_new
    frob_norm = jnp.sqrt(jnp.sum(blended * blended)) + epsilon
    iterate = (blended / frob_norm).astype(jnp.bfloat16)
    result = iterate
    for iteration in range(NS_ITERS):
        gram_matrix = lax.dot_general(
            iterate, iterate, (((1,), (1,)), ((), ())), preferred_element_type=jnp.float32
        ).astype(jnp.bfloat16)
        square = jnp.dot(gram_matrix, gram_matrix, preferred_element_type=jnp.float32)
        polynomial = (
            quintic_two * gram_matrix.astype(jnp.float32) + quintic_three * square
        ).astype(jnp.bfloat16)
        next_iter = quintic_one * iterate.astype(jnp.float32) + jnp.dot(
            polynomial, iterate, preferred_element_type=jnp.float32
        )
        if iteration + 1 < NS_ITERS:
            iterate = next_iter.astype(jnp.bfloat16)
        else:
            result = (math.sqrt(extent) * next_iter).astype(jnp.bfloat16)
    return (result, moment_new)


TILE = 256
QUARTER = 4
TRANSPOSED = (((1,), (1,)), ((), ()))


def newton_schulz_kernel(
    slots_ref, take_ref, m_ref, place_ref, out_ref, mn_ref, g_ref, x0_ref, x1_ref, a_ref, p_ref
):
    extent = g_ref.shape[0]
    tiles = extent // TILE
    slot_total = slots_ref.shape[0]

    def rows_of(i):
        return pl.ds(i * TILE, TILE)

    for i in range(tiles):
        rows = pl.ds(i * TILE, TILE)
        lanes = i * TILE + lax.broadcasted_iota(jnp.int32, (TILE, slot_total - i * TILE), 1)
        chosen = (take_ref[rows, :] == lanes).astype(jnp.bfloat16)
        g_ref[rows, :] = jnp.dot(
            chosen, slots_ref[i * TILE :, :], preferred_element_type=jnp.float32
        ).astype(jnp.bfloat16)

    def moment_tile(i, acc):
        rows = rows_of(i)
        gradient = g_ref[rows, :].astype(jnp.float32)
        moment_new = momentum_decay * m_ref[rows, :] + grad_share * gradient
        mn_ref[rows, :] = moment_new
        blended = grad_share * gradient + momentum_decay * moment_new
        return acc + jnp.sum(blended * blended, axis=0, keepdims=True)

    acc = jnp.zeros((1, extent), jnp.float32)
    for i in range(tiles):
        acc = moment_tile(i, acc)
    frob_norm = jnp.sqrt(jnp.sum(acc, axis=1, keepdims=True)) + epsilon

    def scale_tile(i, carry):
        rows = rows_of(i)
        gradient = g_ref[rows, :].astype(jnp.float32)
        blended = grad_share * gradient + momentum_decay * mn_ref[rows, :]
        x0_ref[rows, :] = (blended / frob_norm).astype(jnp.bfloat16)
        return carry

    for i in range(tiles):
        scale_tile(i, 0)
    iterates = (x0_ref, x1_ref)
    for iteration in range(NS_ITERS):
        now = iterates[iteration % 2]
        later = iterates[(iteration + 1) % 2]
        last = iteration + 1 == NS_ITERS

        for i in range(tiles):
            rows = pl.ds(i * TILE, TILE)
            for j in range(i, tiles):
                cols = pl.ds(j * TILE, TILE)
                block = lax.dot_general(
                    now[rows, :], now[cols, :], TRANSPOSED, preferred_element_type=jnp.float32
                )
                a_ref[rows, cols] = block.astype(jnp.bfloat16)
                if j > i:
                    a_ref[cols, rows] = block.T.astype(jnp.bfloat16)
        for i in range(tiles):
            rows = pl.ds(i * TILE, TILE)
            for j in range(i, tiles):
                cols = pl.ds(j * TILE, TILE)
                square = jnp.dot(a_ref[rows, :], a_ref[:, cols], preferred_element_type=jnp.float32)
                block = quintic_two * a_ref[rows, cols].astype(jnp.float32) + quintic_three * square
                p_ref[rows, cols] = block.astype(jnp.bfloat16)
                if j > i:
                    p_ref[cols, rows] = block.T.astype(jnp.bfloat16)

        def next_tile(i, carry, now=now, later=later, last=last):
            rows = rows_of(i)
            next_iter = quintic_one * now[rows, :].astype(jnp.float32) + jnp.dot(
                p_ref[rows, :], now[...], preferred_element_type=jnp.float32
            )
            if last:
                a_ref[rows, :] = (math.sqrt(extent) * next_iter).astype(jnp.bfloat16)
            else:
                later[rows, :] = next_iter.astype(jnp.bfloat16)
            return carry

        for i in range(tiles):
            next_tile(i, 0)

    chunks, quarter = out_ref.shape[0], out_ref.shape[1]
    span = TILE // quarter
    for i in range(chunks // span):
        reach = min(extent, (i + 1) * TILE)
        lanes = lax.broadcasted_iota(jnp.int32, (span, reach), 1)
        for q in range(quarter):
            rows = pl.ds(q * chunks + i * span, span)
            chosen = (place_ref[rows, :] == lanes).astype(jnp.bfloat16)
            out_ref[pl.ds(i * span, span), q, :] = jnp.dot(
                chosen, a_ref[:reach, :], preferred_element_type=jnp.float32
            ).astype(jnp.bfloat16)


def orthogonalize_kernel(slots, take, moment, place):
    extent = moment.shape[0]
    out_rows = (place.shape[0] // QUARTER, QUARTER, extent)
    square = (extent, extent)
    vmem = pl.BlockSpec(memory_space=pltpu.VMEM)
    return pl.pallas_call(
        newton_schulz_kernel,
        out_shape=(
            jax.ShapeDtypeStruct(out_rows, jnp.bfloat16),
            jax.ShapeDtypeStruct(square, jnp.float32),
        ),
        in_specs=[vmem, vmem, vmem, vmem],
        out_specs=(vmem, vmem),
        scratch_shapes=[pltpu.VMEM(square, jnp.bfloat16) for _ in range(5)],
        compiler_params=pltpu.CompilerParams(vmem_limit_bytes=48 * 1024 * 1024),
        cost_estimate=pl.CostEstimate(
            flops=2 * (3 * NS_ITERS + 2) * extent ** 3,
            bytes_accessed=16 * extent * extent,
            transcendentals=0,
        ),
    )(slots, take, moment, place)


def spare_pair(slots, take, moment, place):
    return (jnp.zeros((place.shape[0] // QUARTER, QUARTER, moment.shape[0]), jnp.bfloat16), jnp.zeros(moment.shape, jnp.float32))


def body(grad_rows, row_counts, owners, momentum):
    matrices, capacity, extent = grad_rows.shape
    shards = lax.axis_size("dp")
    dp_index = lax.axis_index("dp")
    rep_index = lax.axis_index("rep")
    slot_ids = slots_of(owners)
    matrix_ids = jnp.arange(matrices, dtype=jnp.int32)
    owner_ids = jnp.arange(shards, dtype=jnp.int32)
    in_lane = slot_ids == rep_index
    lane_pick = (owners[None, :] == owner_ids[:, None]) & in_lane[None, :]
    lane_matrix = jnp.sum(jnp.where(lane_pick, matrix_ids[None, :], 0), axis=1)
    send_table = jnp.take(grad_rows, lane_matrix, axis=0, mode="clip")
    arrived = lax.all_to_all(send_table, "dp", split_axis=0, concat_axis=0, tiled=True)

    held_here = (owners == dp_index) & in_lane
    active = jnp.any(held_here)
    counts = jnp.sum(jnp.where(held_here[:, None], row_counts, 0), axis=0)
    starts = exclusive_starts(counts)
    row_ids = jnp.arange(extent, dtype=jnp.int32)
    covers = (starts[None, :] <= row_ids[:, None]) & (row_ids[:, None] < (starts + counts)[None, :])
    holder = jnp.sum(jnp.where(covers, owner_ids[None, :], 0), axis=1)
    first_row = jnp.sum(jnp.where(covers, starts[None, :], 0), axis=1)
    row_index = holder * capacity + (row_ids - first_row)
    offsets = jnp.arange(capacity, dtype=jnp.int32)
    positions = starts[:, None] + offsets[None, :]
    usable = offsets[None, :] < counts[:, None]
    place = jnp.where(usable, positions, -1).reshape(-1, QUARTER).T.reshape(shards * capacity, 1)
    take, place, active = lax.optimization_barrier((row_index[:, None], place, active))
    outgoing, moment_new = lax.cond(
        active,
        orthogonalize_kernel,
        spare_pair,
        arrived.reshape(shards * capacity, extent),
        take,
        momentum[0, 0],
        place,
    )
    lanes = lax.axis_size("rep")
    quarter = capacity // lanes
    returned = lax.all_to_all(outgoing, ("dp", "rep"), split_axis=0, concat_axis=0, tiled=True)
    mine = jnp.take(returned.reshape(shards * lanes, quarter, extent), owners * lanes + slot_ids, axis=0, mode="clip")
    def shifted(block, step):
        return lax.ppermute(block, "rep", [(q, (q + step) % lanes) for q in range(lanes)])

    half = quarter // 2
    from_left = shifted(mine, 1)
    from_right = shifted(mine, lanes - 1)
    from_far = jnp.concatenate(
        [shifted(from_left[:, :half], 1), shifted(from_right[:, half:], lanes - 1)], axis=1
    )
    picked_rows = jnp.zeros((matrices, capacity, extent), mine.dtype)
    for shift, block in ((0, mine), (1, from_left), (lanes - 1, from_right), (2, from_far)):
        source = (rep_index - shift + lanes) % lanes
        picked_rows = lax.dynamic_update_slice(picked_rows, block, (0, source * quarter, 0))
    return (picked_rows, moment_new[None, None])


def solution(mesh):
    return jax.shard_map(
        body,
        mesh=mesh,
        in_specs=(P(None, "dp", None), P(), P(), P("dp", "rep", None, None)),
        out_specs=(P(None, "dp", None), P("dp", "rep", None, None)),
        check_vma=False,
    )
```

```python
import math

import jax
import jax.numpy as jnp
from jax import lax
from jax.experimental import pallas as pl
from jax.experimental.pallas import tpu as pltpu
from jax.sharding import PartitionSpec as P

NS_ITERS = 5


momentum_decay = 0.95
grad_share = 0.05
epsilon = 1e-06
quintic_one = 3.4445
quintic_two = -4.775
quintic_three = 2.0315


def slots_of(owners):
    total = owners.shape[0]
    same_owner = owners[:, None] == owners[None, :]
    position = jnp.arange(total, dtype=jnp.int32)
    earlier = position[None, :] < position[:, None]
    return jnp.sum((same_owner & earlier).astype(jnp.int32), axis=1)


def exclusive_starts(counts):
    shards = counts.shape[0]
    ids = jnp.arange(shards, dtype=jnp.int32)
    before = ids[None, :] < ids[:, None]
    return jnp.sum(jnp.where(before, counts[None, :], 0), axis=1)


def orthogonalize(full_grad, moment):
    extent = full_grad.shape[0]
    gradient = full_grad.astype(jnp.float32)
    moment_new = momentum_decay * moment + grad_share * gradient
    blended = grad_share * gradient + momentum_decay * moment_new
    frob_norm = jnp.sqrt(jnp.sum(blended * blended)) + epsilon
    iterate = (blended / frob_norm).astype(jnp.bfloat16)
    result = iterate
    for iteration in range(NS_ITERS):
        gram_matrix = lax.dot_general(
            iterate, iterate, (((1,), (1,)), ((), ())), preferred_element_type=jnp.float32
        ).astype(jnp.bfloat16)
        square = jnp.dot(gram_matrix, gram_matrix, preferred_element_type=jnp.float32)
        polynomial = (
            quintic_two * gram_matrix.astype(jnp.float32) + quintic_three * square
        ).astype(jnp.bfloat16)
        next_iter = quintic_one * iterate.astype(jnp.float32) + jnp.dot(
            polynomial, iterate, preferred_element_type=jnp.float32
        )
        if iteration + 1 < NS_ITERS:
            iterate = next_iter.astype(jnp.bfloat16)
        else:
            result = (math.sqrt(extent) * next_iter).astype(jnp.bfloat16)
    return (result, moment_new)


TILE = 256
QUARTER = 4
TRANSPOSED = (((1,), (1,)), ((), ()))


def newton_schulz_kernel(
    slots_ref, take_ref, m_ref, place_ref, out_ref, mn_ref, g_ref, x0_ref, x1_ref, a_ref, p_ref
):
    extent = g_ref.shape[0]
    tiles = extent // TILE
    slot_total = slots_ref.shape[0]

    def rows_of(i):
        return pl.ds(i * TILE, TILE)

    for i in range(tiles):
        rows = pl.ds(i * TILE, TILE)
        lanes = i * TILE + lax.broadcasted_iota(jnp.int32, (TILE, slot_total - i * TILE), 1)
        chosen = (take_ref[rows, :] == lanes).astype(jnp.bfloat16)
        g_ref[rows, :] = jnp.dot(
            chosen, slots_ref[i * TILE :, :], preferred_element_type=jnp.float32
        ).astype(jnp.bfloat16)

    def moment_tile(i, acc):
        rows = rows_of(i)
        gradient = g_ref[rows, :].astype(jnp.float32)
        moment_new = momentum_decay * m_ref[rows, :] + grad_share * gradient
        mn_ref[rows, :] = moment_new
        blended = grad_share * gradient + momentum_decay * moment_new
        return acc + jnp.sum(blended * blended, axis=0, keepdims=True)

    acc = jnp.zeros((1, extent), jnp.float32)
    for i in range(tiles):
        acc = moment_tile(i, acc)
    frob_norm = jnp.sqrt(jnp.sum(acc, axis=1, keepdims=True)) + epsilon

    def scale_tile(i, carry):
        rows = rows_of(i)
        gradient = g_ref[rows, :].astype(jnp.float32)
        blended = grad_share * gradient + momentum_decay * mn_ref[rows, :]
        x0_ref[rows, :] = (blended / frob_norm).astype(jnp.bfloat16)
        return carry

    for i in range(tiles):
        scale_tile(i, 0)
    iterates = (x0_ref, x1_ref)
    for iteration in range(NS_ITERS):
        now = iterates[iteration % 2]
        later = iterates[(iteration + 1) % 2]
        last = iteration + 1 == NS_ITERS

        for i in range(tiles):
            rows = pl.ds(i * TILE, TILE)
            for j in range(i, tiles):
                cols = pl.ds(j * TILE, TILE)
                block = lax.dot_general(
                    now[rows, :], now[cols, :], TRANSPOSED, preferred_element_type=jnp.float32
                )
                a_ref[rows, cols] = block.astype(jnp.bfloat16)
                if j > i:
                    a_ref[cols, rows] = block.T.astype(jnp.bfloat16)
        for i in range(tiles):
            rows = pl.ds(i * TILE, TILE)
            for j in range(i, tiles):
                cols = pl.ds(j * TILE, TILE)
                square = jnp.dot(a_ref[rows, :], a_ref[:, cols], preferred_element_type=jnp.float32)
                block = quintic_two * a_ref[rows, cols].astype(jnp.float32) + quintic_three * square
                p_ref[rows, cols] = block.astype(jnp.bfloat16)
                if j > i:
                    p_ref[cols, rows] = block.T.astype(jnp.bfloat16)

        def next_tile(i, carry, now=now, later=later, last=last):
            rows = rows_of(i)
            next_iter = quintic_one * now[rows, :].astype(jnp.float32) + jnp.dot(
                p_ref[rows, :], now[...], preferred_element_type=jnp.float32
            )
            if last:
                a_ref[rows, :] = (math.sqrt(extent) * next_iter).astype(jnp.bfloat16)
            else:
                later[rows, :] = next_iter.astype(jnp.bfloat16)
            return carry

        for i in range(tiles):
            next_tile(i, 0)

    chunks, quarter = out_ref.shape[0], out_ref.shape[1]
    span = TILE // quarter
    for i in range(chunks // span):
        reach = min(extent, (i + 1) * TILE)
        lanes = lax.broadcasted_iota(jnp.int32, (TILE, reach), 1)
        chosen = (place_ref[pl.ds(i * TILE, TILE), :] == lanes).astype(jnp.bfloat16)
        placed = jnp.dot(chosen, a_ref[:reach, :], preferred_element_type=jnp.float32)
        for q in range(quarter):
            out_ref[pl.ds(i * span, span), q, :] = placed[q * span : (q + 1) * span].astype(jnp.bfloat16)


def orthogonalize_kernel(slots, take, moment, place):
    extent = moment.shape[0]
    out_rows = (place.shape[0] // QUARTER, QUARTER, extent)
    square = (extent, extent)
    vmem = pl.BlockSpec(memory_space=pltpu.VMEM)
    return pl.pallas_call(
        newton_schulz_kernel,
        out_shape=(
            jax.ShapeDtypeStruct(out_rows, jnp.bfloat16),
            jax.ShapeDtypeStruct(square, jnp.float32),
        ),
        in_specs=[vmem, vmem, vmem, vmem],
        out_specs=(vmem, vmem),
        scratch_shapes=[pltpu.VMEM(square, jnp.bfloat16) for _ in range(5)],
        compiler_params=pltpu.CompilerParams(vmem_limit_bytes=48 * 1024 * 1024),
        cost_estimate=pl.CostEstimate(
            flops=2 * (3 * NS_ITERS + 2) * extent ** 3,
            bytes_accessed=16 * extent * extent,
            transcendentals=0,
        ),
    )(slots, take, moment, place)


def spare_pair(slots, take, moment, place):
    return (jnp.zeros((place.shape[0] // QUARTER, QUARTER, moment.shape[0]), jnp.bfloat16), jnp.zeros(moment.shape, jnp.float32))


def body(grad_rows, row_counts, owners, momentum):
    matrices, capacity, extent = grad_rows.shape
    shards = lax.axis_size("dp")
    dp_index = lax.axis_index("dp")
    rep_index = lax.axis_index("rep")
    slot_ids = slots_of(owners)
    matrix_ids = jnp.arange(matrices, dtype=jnp.int32)
    owner_ids = jnp.arange(shards, dtype=jnp.int32)
    in_lane = slot_ids == rep_index
    lane_pick = (owners[None, :] == owner_ids[:, None]) & in_lane[None, :]
    lane_matrix = jnp.sum(jnp.where(lane_pick, matrix_ids[None, :], 0), axis=1)
    send_table = jnp.take(grad_rows, lane_matrix, axis=0, mode="clip")
    arrived = lax.all_to_all(send_table, "dp", split_axis=0, concat_axis=0, tiled=True)

    held_here = (owners == dp_index) & in_lane
    active = jnp.any(held_here)
    counts = jnp.sum(jnp.where(held_here[:, None], row_counts, 0), axis=0)
    starts = exclusive_starts(counts)
    row_ids = jnp.arange(extent, dtype=jnp.int32)
    covers = (starts[None, :] <= row_ids[:, None]) & (row_ids[:, None] < (starts + counts)[None, :])
    holder = jnp.sum(jnp.where(covers, owner_ids[None, :], 0), axis=1)
    first_row = jnp.sum(jnp.where(covers, starts[None, :], 0), axis=1)
    row_index = holder * capacity + (row_ids - first_row)
    offsets = jnp.arange(capacity, dtype=jnp.int32)
    positions = starts[:, None] + offsets[None, :]
    usable = offsets[None, :] < counts[:, None]
    place = jnp.where(usable, positions, -1).reshape(-1, TILE // QUARTER, QUARTER)
    place = jnp.swapaxes(place, 1, 2).reshape(shards * capacity, 1)
    take, place, active = lax.optimization_barrier((row_index[:, None], place, active))
    outgoing, moment_new = lax.cond(
        active,
        orthogonalize_kernel,
        spare_pair,
        arrived.reshape(shards * capacity, extent),
        take,
        momentum[0, 0],
        place,
    )
    lanes = lax.axis_size("rep")
    quarter = capacity // lanes
    returned = lax.all_to_all(outgoing, ("dp", "rep"), split_axis=0, concat_axis=0, tiled=True)
    mine = jnp.take(returned.reshape(shards * lanes, quarter, extent), owners * lanes + slot_ids, axis=0, mode="clip")
    def shifted(block, step):
        return lax.ppermute(block, "rep", [(q, (q + step) % lanes) for q in range(lanes)])

    half = quarter // 2
    from_left = shifted(mine, 1)
    from_right = shifted(mine, lanes - 1)
    from_far = jnp.concatenate(
        [shifted(from_left[:, :half], 1), shifted(from_right[:, half:], lanes - 1)], axis=1
    )
    picked_rows = jnp.zeros((matrices, capacity, extent), mine.dtype)
    for shift, block in ((0, mine), (1, from_left), (lanes - 1, from_right), (2, from_far)):
        source = (rep_index - shift + lanes) % lanes
        picked_rows = lax.dynamic_update_slice(picked_rows, block, (0, source * quarter, 0))
    return (picked_rows, moment_new[None, None])


def solution(mesh):
    return jax.shard_map(
        body,
        mesh=mesh,
        in_specs=(P(None, "dp", None), P(), P(), P("dp", "rep", None, None)),
        out_specs=(P(None, "dp", None), P("dp", "rep", None, None)),
        check_vma=False,
    )
```

```python
import math

import jax
import jax.numpy as jnp
from jax import lax
from jax.experimental import pallas as pl
from jax.experimental.pallas import tpu as pltpu
from jax.sharding import PartitionSpec as P

NS_ITERS = 5


momentum_decay = 0.95
grad_share = 0.05
epsilon = 1e-06
quintic_one = 3.4445
quintic_two = -4.775
quintic_three = 2.0315


def slots_of(owners):
    total = owners.shape[0]
    same_owner = owners[:, None] == owners[None, :]
    position = jnp.arange(total, dtype=jnp.int32)
    earlier = position[None, :] < position[:, None]
    return jnp.sum((same_owner & earlier).astype(jnp.int32), axis=1)


def exclusive_starts(counts):
    shards = counts.shape[0]
    ids = jnp.arange(shards, dtype=jnp.int32)
    before = ids[None, :] < ids[:, None]
    return jnp.sum(jnp.where(before, counts[None, :], 0), axis=1)


def orthogonalize(full_grad, moment):
    extent = full_grad.shape[0]
    gradient = full_grad.astype(jnp.float32)
    moment_new = momentum_decay * moment + grad_share * gradient
    blended = grad_share * gradient + momentum_decay * moment_new
    frob_norm = jnp.sqrt(jnp.sum(blended * blended)) + epsilon
    iterate = (blended / frob_norm).astype(jnp.bfloat16)
    result = iterate
    for iteration in range(NS_ITERS):
        gram_matrix = lax.dot_general(
            iterate, iterate, (((1,), (1,)), ((), ())), preferred_element_type=jnp.float32
        ).astype(jnp.bfloat16)
        square = jnp.dot(gram_matrix, gram_matrix, preferred_element_type=jnp.float32)
        polynomial = (
            quintic_two * gram_matrix.astype(jnp.float32) + quintic_three * square
        ).astype(jnp.bfloat16)
        next_iter = quintic_one * iterate.astype(jnp.float32) + jnp.dot(
            polynomial, iterate, preferred_element_type=jnp.float32
        )
        if iteration + 1 < NS_ITERS:
            iterate = next_iter.astype(jnp.bfloat16)
        else:
            result = (math.sqrt(extent) * next_iter).astype(jnp.bfloat16)
    return (result, moment_new)


TILE = 256
QUARTER = 4
TRANSPOSED = (((1,), (1,)), ((), ()))


def newton_schulz_kernel(
    slots_ref, take_ref, m_ref, place_ref, out_ref, mn_ref, g_ref, x0_ref, x1_ref, a_ref, p_ref
):
    extent = g_ref.shape[0]
    tiles = extent // TILE
    slot_total = slots_ref.shape[0]

    def rows_of(i):
        return pl.ds(i * TILE, TILE)

    for i in range(tiles):
        rows = pl.ds(i * TILE, TILE)
        lanes = i * TILE + lax.broadcasted_iota(jnp.int32, (TILE, slot_total - i * TILE), 1)
        chosen = (take_ref[rows, :] == lanes).astype(jnp.bfloat16)
        g_ref[rows, :] = jnp.dot(
            chosen, slots_ref[i * TILE :, :], preferred_element_type=jnp.float32
        ).astype(jnp.bfloat16)

    def moment_tile(i, acc):
        rows = rows_of(i)
        gradient = g_ref[rows, :].astype(jnp.float32)
        moment_new = momentum_decay * m_ref[rows, :] + grad_share * gradient
        mn_ref[rows, :] = moment_new
        blended = grad_share * gradient + momentum_decay * moment_new
        return acc + jnp.sum(blended * blended, axis=0, keepdims=True)

    acc = jnp.zeros((1, extent), jnp.float32)
    for i in range(tiles):
        acc = moment_tile(i, acc)
    frob_norm = jnp.sqrt(jnp.sum(acc, axis=1, keepdims=True)) + epsilon

    def scale_tile(i, carry):
        rows = rows_of(i)
        gradient = g_ref[rows, :].astype(jnp.float32)
        blended = grad_share * gradient + momentum_decay * mn_ref[rows, :]
        x0_ref[rows, :] = (blended / frob_norm).astype(jnp.bfloat16)
        return carry

    for i in range(tiles):
        scale_tile(i, 0)
    iterates = (x0_ref, x1_ref)
    for iteration in range(NS_ITERS):
        now = iterates[iteration % 2]
        later = iterates[(iteration + 1) % 2]
        last = iteration + 1 == NS_ITERS

        for i in range(tiles):
            rows = pl.ds(i * TILE, TILE)
            for j in range(i, tiles):
                cols = pl.ds(j * TILE, TILE)
                block = lax.dot_general(
                    now[rows, :], now[cols, :], TRANSPOSED, preferred_element_type=jnp.float32
                )
                a_ref[rows, cols] = block.astype(jnp.bfloat16)
                if j > i:
                    a_ref[cols, rows] = block.T.astype(jnp.bfloat16)
        for i in range(tiles):
            rows = pl.ds(i * TILE, TILE)
            for j in range(i, tiles):
                cols = pl.ds(j * TILE, TILE)
                square = jnp.dot(a_ref[rows, :], a_ref[:, cols], preferred_element_type=jnp.float32)
                block = quintic_two * a_ref[rows, cols].astype(jnp.float32) + quintic_three * square
                p_ref[rows, cols] = block.astype(jnp.bfloat16)
                if j > i:
                    p_ref[cols, rows] = block.T.astype(jnp.bfloat16)

        def next_tile(i, carry, now=now, later=later, last=last):
            rows = rows_of(i)
            next_iter = quintic_one * now[rows, :].astype(jnp.float32) + jnp.dot(
                p_ref[rows, :], now[...], preferred_element_type=jnp.float32
            )
            if last:
                a_ref[rows, :] = (math.sqrt(extent) * next_iter).astype(jnp.bfloat16)
            else:
                later[rows, :] = next_iter.astype(jnp.bfloat16)
            return carry

        for i in range(tiles):
            next_tile(i, 0)

    chunks, quarter = out_ref.shape[0], out_ref.shape[1]
    span = TILE // quarter
    for i in range(chunks // span):
        reach = min(extent, (i + 1) * TILE)
        lanes = lax.broadcasted_iota(jnp.int32, (TILE, reach), 1)
        chosen = (place_ref[pl.ds(i * TILE, TILE), :] == lanes).astype(jnp.bfloat16)
        placed = jnp.dot(chosen, a_ref[:reach, :], preferred_element_type=jnp.float32)
        for q in range(quarter):
            out_ref[pl.ds(i * span, span), q, :] = placed[q * span : (q + 1) * span].astype(jnp.bfloat16)


def orthogonalize_kernel(slots, take, moment, place):
    extent = moment.shape[0]
    out_rows = (place.shape[0] // QUARTER, QUARTER, extent)
    square = (extent, extent)
    vmem = pl.BlockSpec(memory_space=pltpu.VMEM)
    return pl.pallas_call(
        newton_schulz_kernel,
        out_shape=(
            jax.ShapeDtypeStruct(out_rows, jnp.bfloat16),
            jax.ShapeDtypeStruct(square, jnp.float32),
        ),
        in_specs=[vmem, vmem, vmem, vmem],
        out_specs=(vmem, vmem),
        scratch_shapes=[pltpu.VMEM(square, jnp.bfloat16) for _ in range(5)],
        compiler_params=pltpu.CompilerParams(vmem_limit_bytes=48 * 1024 * 1024),
        cost_estimate=pl.CostEstimate(
            flops=2 * (3 * NS_ITERS + 2) * extent ** 3,
            bytes_accessed=16 * extent * extent,
            transcendentals=0,
        ),
    )(slots, take, moment, place)


def spare_pair(slots, take, moment, place):
    return (jnp.zeros((place.shape[0] // QUARTER, QUARTER, moment.shape[0]), jnp.bfloat16), jnp.zeros(moment.shape, jnp.float32))


def body(grad_rows, row_counts, owners, momentum):
    matrices, capacity, extent = grad_rows.shape
    shards = lax.axis_size("dp")
    dp_index = lax.axis_index("dp")
    rep_index = lax.axis_index("rep")
    slot_ids = slots_of(owners)
    matrix_ids = jnp.arange(matrices, dtype=jnp.int32)
    owner_ids = jnp.arange(shards, dtype=jnp.int32)
    in_lane = slot_ids == rep_index
    owned = owners[None, :] == owner_ids[:, None]
    earlier = (matrix_ids[:, None] < matrix_ids[None, :]).astype(jnp.float32)
    seen = jnp.dot(owned.astype(jnp.float32), earlier, precision=lax.Precision.HIGHEST)
    lane_pick = owned & (seen == rep_index.astype(jnp.float32))
    lane_matrix = jnp.sum(jnp.where(lane_pick, matrix_ids[None, :], 0), axis=1)
    send_table = jnp.take(grad_rows, lane_matrix, axis=0, mode="clip")
    arrived = lax.all_to_all(send_table, "dp", split_axis=0, concat_axis=0, tiled=True)

    held_here = (owners == dp_index) & in_lane
    active = jnp.any(held_here)
    counts = jnp.sum(jnp.where(held_here[:, None], row_counts, 0), axis=0)
    starts = exclusive_starts(counts)
    row_ids = jnp.arange(extent, dtype=jnp.int32)
    covers = (starts[None, :] <= row_ids[:, None]) & (row_ids[:, None] < (starts + counts)[None, :])
    holder = jnp.sum(jnp.where(covers, owner_ids[None, :], 0), axis=1)
    first_row = jnp.sum(jnp.where(covers, starts[None, :], 0), axis=1)
    row_index = holder * capacity + (row_ids - first_row)
    offsets = jnp.arange(capacity, dtype=jnp.int32)
    positions = starts[:, None] + offsets[None, :]
    usable = offsets[None, :] < counts[:, None]
    place = jnp.where(usable, positions, -1).reshape(-1, TILE // QUARTER, QUARTER)
    place = jnp.swapaxes(place, 1, 2).reshape(shards * capacity, 1)
    take, place, active = lax.optimization_barrier((row_index[:, None], place, active))
    outgoing, moment_new = lax.cond(
        active,
        orthogonalize_kernel,
        spare_pair,
        arrived.reshape(shards * capacity, extent),
        take,
        momentum[0, 0],
        place,
    )
    lanes = lax.axis_size("rep")
    quarter = capacity // lanes
    returned = lax.all_to_all(outgoing, ("dp", "rep"), split_axis=0, concat_axis=0, tiled=True)
    mine = jnp.take(returned.reshape(shards * lanes, quarter, extent), owners * lanes + slot_ids, axis=0, mode="clip")
    def shifted(block, step):
        return lax.ppermute(block, "rep", [(q, (q + step) % lanes) for q in range(lanes)])

    half = quarter // 2
    from_left = shifted(mine, 1)
    from_right = shifted(mine, lanes - 1)
    from_far = jnp.concatenate(
        [shifted(from_left[:, :half], 1), shifted(from_right[:, half:], lanes - 1)], axis=1
    )
    picked_rows = jnp.zeros((matrices, capacity, extent), mine.dtype)
    for shift, block in ((0, mine), (1, from_left), (lanes - 1, from_right), (2, from_far)):
        source = (rep_index - shift + lanes) % lanes
        picked_rows = lax.dynamic_update_slice(picked_rows, block, (0, source * quarter, 0))
    return (picked_rows, moment_new[None, None])


def solution(mesh):
    return jax.shard_map(
        body,
        mesh=mesh,
        in_specs=(P(None, "dp", None), P(), P(), P("dp", "rep", None, None)),
        out_specs=(P(None, "dp", None), P("dp", "rep", None, None)),
        check_vma=False,
    )
```

```python
import math

import jax
import jax.numpy as jnp
from jax import lax
from jax.experimental import pallas as pl
from jax.experimental.pallas import tpu as pltpu
from jax.sharding import PartitionSpec as P

NS_ITERS = 5


momentum_decay = 0.95
grad_share = 0.05
epsilon = 1e-06
quintic_one = 3.4445
quintic_two = -4.775
quintic_three = 2.0315


def slots_of(owners):
    total = owners.shape[0]
    same_owner = owners[:, None] == owners[None, :]
    position = jnp.arange(total, dtype=jnp.int32)
    earlier = position[None, :] < position[:, None]
    return jnp.sum((same_owner & earlier).astype(jnp.int32), axis=1)


def exclusive_starts(counts):
    shards = counts.shape[0]
    ids = jnp.arange(shards, dtype=jnp.int32)
    before = ids[None, :] < ids[:, None]
    return jnp.sum(jnp.where(before, counts[None, :], 0), axis=1)


def orthogonalize(full_grad, moment):
    extent = full_grad.shape[0]
    gradient = full_grad.astype(jnp.float32)
    moment_new = momentum_decay * moment + grad_share * gradient
    blended = grad_share * gradient + momentum_decay * moment_new
    frob_norm = jnp.sqrt(jnp.sum(blended * blended)) + epsilon
    iterate = (blended / frob_norm).astype(jnp.bfloat16)
    result = iterate
    for iteration in range(NS_ITERS):
        gram_matrix = lax.dot_general(
            iterate, iterate, (((1,), (1,)), ((), ())), preferred_element_type=jnp.float32
        ).astype(jnp.bfloat16)
        square = jnp.dot(gram_matrix, gram_matrix, preferred_element_type=jnp.float32)
        polynomial = (
            quintic_two * gram_matrix.astype(jnp.float32) + quintic_three * square
        ).astype(jnp.bfloat16)
        next_iter = quintic_one * iterate.astype(jnp.float32) + jnp.dot(
            polynomial, iterate, preferred_element_type=jnp.float32
        )
        if iteration + 1 < NS_ITERS:
            iterate = next_iter.astype(jnp.bfloat16)
        else:
            result = (math.sqrt(extent) * next_iter).astype(jnp.bfloat16)
    return (result, moment_new)


TILE = 256
QUARTER = 4
TRANSPOSED = (((1,), (1,)), ((), ()))


def newton_schulz_kernel(
    slots_ref, take_ref, m_ref, place_ref, out_ref, mn_ref, g_ref, x0_ref, x1_ref, a_ref, p_ref
):
    extent = g_ref.shape[0]
    tiles = extent // TILE
    slot_total = slots_ref.shape[0]

    def rows_of(i):
        return pl.ds(i * TILE, TILE)

    for i in range(tiles):
        rows = pl.ds(i * TILE, TILE)
        lanes = i * TILE + lax.broadcasted_iota(jnp.int32, (TILE, slot_total - i * TILE), 1)
        chosen = (take_ref[rows, :] == lanes).astype(jnp.bfloat16)
        g_ref[rows, :] = jnp.dot(
            chosen, slots_ref[i * TILE :, :], preferred_element_type=jnp.float32
        ).astype(jnp.bfloat16)

    def moment_tile(i, acc):
        rows = rows_of(i)
        gradient = g_ref[rows, :].astype(jnp.float32)
        moment_new = momentum_decay * m_ref[rows, :] + grad_share * gradient
        mn_ref[rows, :] = moment_new
        blended = grad_share * gradient + momentum_decay * moment_new
        return acc + jnp.sum(blended * blended, axis=0, keepdims=True)

    acc = jnp.zeros((1, extent), jnp.float32)
    for i in range(tiles):
        acc = moment_tile(i, acc)
    frob_norm = jnp.sqrt(jnp.sum(acc, axis=1, keepdims=True)) + epsilon

    def scale_tile(i, carry):
        rows = rows_of(i)
        gradient = g_ref[rows, :].astype(jnp.float32)
        blended = grad_share * gradient + momentum_decay * mn_ref[rows, :]
        x0_ref[rows, :] = (blended / frob_norm).astype(jnp.bfloat16)
        return carry

    for i in range(tiles):
        scale_tile(i, 0)
    iterates = (x0_ref, x1_ref)
    for iteration in range(NS_ITERS):
        now = iterates[iteration % 2]
        later = iterates[(iteration + 1) % 2]
        last = iteration + 1 == NS_ITERS

        for i in range(tiles):
            rows = pl.ds(i * TILE, TILE)
            for j in range(i, tiles):
                cols = pl.ds(j * TILE, TILE)
                block = lax.dot_general(
                    now[rows, :], now[cols, :], TRANSPOSED, preferred_element_type=jnp.float32
                )
                a_ref[rows, cols] = block.astype(jnp.bfloat16)
                if j > i:
                    a_ref[cols, rows] = block.T.astype(jnp.bfloat16)
        for i in range(tiles):
            rows = pl.ds(i * TILE, TILE)
            for j in range(i, tiles):
                cols = pl.ds(j * TILE, TILE)
                square = jnp.dot(a_ref[rows, :], a_ref[:, cols], preferred_element_type=jnp.float32)
                block = quintic_two * a_ref[rows, cols].astype(jnp.float32) + quintic_three * square
                p_ref[rows, cols] = block.astype(jnp.bfloat16)
                if j > i:
                    p_ref[cols, rows] = block.T.astype(jnp.bfloat16)

        def next_tile(i, carry, now=now, later=later, last=last):
            rows = rows_of(i)
            next_iter = quintic_one * now[rows, :].astype(jnp.float32) + jnp.dot(
                p_ref[rows, :], now[...], preferred_element_type=jnp.float32
            )
            if last:
                a_ref[rows, :] = (math.sqrt(extent) * next_iter).astype(jnp.bfloat16)
            else:
                later[rows, :] = next_iter.astype(jnp.bfloat16)
            return carry

        for i in range(tiles):
            next_tile(i, 0)

    chunks, quarter = out_ref.shape[0], out_ref.shape[1]
    span = TILE // quarter
    for i in range(chunks // span):
        reach = min(extent, (i + 1) * TILE)
        lanes = lax.broadcasted_iota(jnp.int32, (TILE, reach), 1)
        chosen = (place_ref[pl.ds(i * TILE, TILE), :] == lanes).astype(jnp.bfloat16)
        placed = jnp.dot(chosen, a_ref[:reach, :], preferred_element_type=jnp.float32)
        for q in range(quarter):
            out_ref[pl.ds(i * span, span), q, :] = placed[q * span : (q + 1) * span].astype(jnp.bfloat16)


def orthogonalize_kernel(slots, take, moment, place):
    extent = moment.shape[0]
    out_rows = (place.shape[0] // QUARTER, QUARTER, extent)
    square = (extent, extent)
    vmem = pl.BlockSpec(memory_space=pltpu.VMEM)
    return pl.pallas_call(
        newton_schulz_kernel,
        out_shape=(
            jax.ShapeDtypeStruct(out_rows, jnp.bfloat16),
            jax.ShapeDtypeStruct(square, jnp.float32),
        ),
        in_specs=[vmem, vmem, vmem, vmem],
        out_specs=(vmem, vmem),
        scratch_shapes=[pltpu.VMEM(square, jnp.bfloat16) for _ in range(5)],
        compiler_params=pltpu.CompilerParams(vmem_limit_bytes=48 * 1024 * 1024),
        cost_estimate=pl.CostEstimate(
            flops=2 * (3 * NS_ITERS + 2) * extent ** 3,
            bytes_accessed=16 * extent * extent,
            transcendentals=0,
        ),
    )(slots, take, moment, place)


def spare_pair(slots, take, moment, place):
    return (jnp.zeros((place.shape[0] // QUARTER, QUARTER, moment.shape[0]), jnp.bfloat16), jnp.zeros(moment.shape, jnp.float32))


def body(grad_rows, row_counts, owners, momentum):
    matrices, capacity, extent = grad_rows.shape
    shards = lax.axis_size("dp")
    dp_index = lax.axis_index("dp")
    rep_index = lax.axis_index("rep")
    slot_ids = slots_of(owners)
    matrix_ids = jnp.arange(matrices, dtype=jnp.int32)
    owner_ids = jnp.arange(shards, dtype=jnp.int32)
    in_lane = slot_ids == rep_index
    owned = owners[None, :] == owner_ids[:, None]
    earlier = (matrix_ids[:, None] < matrix_ids[None, :]).astype(jnp.float32)
    seen = jnp.dot(owned.astype(jnp.float32), earlier, precision=lax.Precision.HIGHEST)
    lane_pick = owned & (seen == rep_index.astype(jnp.float32))
    lane_matrix = jnp.sum(jnp.where(lane_pick, matrix_ids[None, :], 0), axis=1)
    send_table = jnp.take(grad_rows, lane_matrix, axis=0, mode="clip")
    arrived = lax.all_to_all(send_table, "dp", split_axis=0, concat_axis=0, tiled=True)

    held_here = (owners == dp_index) & in_lane
    active = jnp.any(held_here)
    counts = jnp.sum(jnp.where(held_here[:, None], row_counts, 0), axis=0)
    starts = exclusive_starts(counts)
    row_ids = jnp.arange(extent, dtype=jnp.int32)
    covers = (starts[None, :] <= row_ids[:, None]) & (row_ids[:, None] < (starts + counts)[None, :])
    holder = jnp.sum(jnp.where(covers, owner_ids[None, :], 0), axis=1)
    first_row = jnp.sum(jnp.where(covers, starts[None, :], 0), axis=1)
    row_index = holder * capacity + (row_ids - first_row)
    offsets = jnp.arange(capacity, dtype=jnp.int32)
    positions = starts[:, None] + offsets[None, :]
    usable = offsets[None, :] < counts[:, None]
    place = jnp.where(usable, positions, -1).reshape(-1, TILE // QUARTER, QUARTER)
    place = jnp.swapaxes(place, 1, 2).reshape(shards * capacity, 1)
    take, place, active = lax.optimization_barrier((row_index[:, None], place, active))
    outgoing, moment_new = lax.cond(
        active,
        orthogonalize_kernel,
        spare_pair,
        arrived.reshape(shards * capacity, extent),
        take,
        momentum[0, 0],
        place,
    )
    lanes = lax.axis_size("rep")
    quarter = capacity // lanes
    returned = lax.all_to_all(outgoing, ("dp", "rep"), split_axis=0, concat_axis=0, tiled=True)
    mine = jnp.take(returned.reshape(shards * lanes, quarter, extent), owners * lanes + slot_ids, axis=0, mode="clip")
    def shifted(block, step):
        return lax.ppermute(block, "rep", [(q, (q + step) % lanes) for q in range(lanes)])

    half = quarter // 2
    from_left = shifted(mine, 1)
    from_right = shifted(mine, lanes - 1)
    from_far = jnp.concatenate(
        [shifted(mine[:, :half], 2), shifted(mine[:, half:], lanes - 2)], axis=1
    )
    picked_rows = jnp.zeros((matrices, capacity, extent), mine.dtype)
    for shift, block in ((0, mine), (1, from_left), (lanes - 1, from_right), (2, from_far)):
        source = (rep_index - shift + lanes) % lanes
        picked_rows = lax.dynamic_update_slice(picked_rows, block, (0, source * quarter, 0))
    return (picked_rows, moment_new[None, None])


def solution(mesh):
    return jax.shard_map(
        body,
        mesh=mesh,
        in_specs=(P(None, "dp", None), P(), P(), P("dp", "rep", None, None)),
        out_specs=(P(None, "dp", None), P("dp", "rep", None, None)),
        check_vma=False,
    )
```

```python
import math

import jax
import jax.numpy as jnp
from jax import lax
from jax.experimental import pallas as pl
from jax.experimental.pallas import tpu as pltpu
from jax.sharding import PartitionSpec as P

NS_ITERS = 5


momentum_decay = 0.95
grad_share = 0.05
epsilon = 1e-06
quintic_one = 3.4445
quintic_two = -4.775
quintic_three = 2.0315


def slots_of(owners):
    total = owners.shape[0]
    same_owner = owners[:, None] == owners[None, :]
    position = jnp.arange(total, dtype=jnp.int32)
    earlier = position[None, :] < position[:, None]
    return jnp.sum((same_owner & earlier).astype(jnp.int32), axis=1)


def exclusive_starts(counts):
    shards = counts.shape[0]
    ids = jnp.arange(shards, dtype=jnp.int32)
    before = ids[None, :] < ids[:, None]
    return jnp.sum(jnp.where(before, counts[None, :], 0), axis=1)


def orthogonalize(full_grad, moment):
    extent = full_grad.shape[0]
    gradient = full_grad.astype(jnp.float32)
    moment_new = momentum_decay * moment + grad_share * gradient
    blended = grad_share * gradient + momentum_decay * moment_new
    frob_norm = jnp.sqrt(jnp.sum(blended * blended)) + epsilon
    iterate = (blended / frob_norm).astype(jnp.bfloat16)
    result = iterate
    for iteration in range(NS_ITERS):
        gram_matrix = lax.dot_general(
            iterate, iterate, (((1,), (1,)), ((), ())), preferred_element_type=jnp.float32
        ).astype(jnp.bfloat16)
        square = jnp.dot(gram_matrix, gram_matrix, preferred_element_type=jnp.float32)
        polynomial = (
            quintic_two * gram_matrix.astype(jnp.float32) + quintic_three * square
        ).astype(jnp.bfloat16)
        next_iter = quintic_one * iterate.astype(jnp.float32) + jnp.dot(
            polynomial, iterate, preferred_element_type=jnp.float32
        )
        if iteration + 1 < NS_ITERS:
            iterate = next_iter.astype(jnp.bfloat16)
        else:
            result = (math.sqrt(extent) * next_iter).astype(jnp.bfloat16)
    return (result, moment_new)


TILE = 256
QUARTER = 4
TRANSPOSED = (((1,), (1,)), ((), ()))


def newton_schulz_kernel(
    slots_ref, take_ref, m_ref, place_ref, out_ref, mn_ref, g_ref, x0_ref, x1_ref, a_ref, p_ref
):
    extent = g_ref.shape[0]
    tiles = extent // TILE
    slot_total = slots_ref.shape[0]

    def rows_of(i):
        return pl.ds(i * TILE, TILE)

    for i in range(tiles):
        rows = pl.ds(i * TILE, TILE)
        lanes = i * TILE + lax.broadcasted_iota(jnp.int32, (TILE, slot_total - i * TILE), 1)
        chosen = (take_ref[rows, :] == lanes).astype(jnp.bfloat16)
        g_ref[rows, :] = jnp.dot(
            chosen, slots_ref[i * TILE :, :], preferred_element_type=jnp.float32
        ).astype(jnp.bfloat16)

    def moment_tile(i, acc):
        rows = rows_of(i)
        gradient = g_ref[rows, :].astype(jnp.float32)
        moment_new = momentum_decay * m_ref[rows, :] + grad_share * gradient
        mn_ref[rows, :] = moment_new
        blended = grad_share * gradient + momentum_decay * moment_new
        return acc + jnp.sum(blended * blended, axis=0, keepdims=True)

    acc = jnp.zeros((1, extent), jnp.float32)
    for i in range(tiles):
        acc = moment_tile(i, acc)
    frob_norm = jnp.sqrt(jnp.sum(acc, axis=1, keepdims=True)) + epsilon

    def scale_tile(i, carry):
        rows = rows_of(i)
        gradient = g_ref[rows, :].astype(jnp.float32)
        blended = grad_share * gradient + momentum_decay * mn_ref[rows, :]
        x0_ref[rows, :] = (blended / frob_norm).astype(jnp.bfloat16)
        return carry

    for i in range(tiles):
        scale_tile(i, 0)
    iterates = (x0_ref, x1_ref)
    for iteration in range(NS_ITERS):
        now = iterates[iteration % 2]
        later = iterates[(iteration + 1) % 2]
        last = iteration + 1 == NS_ITERS

        for i in range(tiles):
            rows = pl.ds(i * TILE, TILE)
            for j in range(i, tiles):
                cols = pl.ds(j * TILE, TILE)
                block = lax.dot_general(
                    now[rows, :], now[cols, :], TRANSPOSED, preferred_element_type=jnp.float32
                )
                a_ref[rows, cols] = block.astype(jnp.bfloat16)
                if j > i:
                    a_ref[cols, rows] = block.T.astype(jnp.bfloat16)
        for i in range(tiles):
            rows = pl.ds(i * TILE, TILE)
            for j in range(i, tiles):
                cols = pl.ds(j * TILE, TILE)
                square = jnp.dot(a_ref[rows, :], a_ref[:, cols], preferred_element_type=jnp.float32)
                block = quintic_two * a_ref[rows, cols].astype(jnp.float32) + quintic_three * square
                p_ref[rows, cols] = block.astype(jnp.bfloat16)
                if j > i:
                    p_ref[cols, rows] = block.T.astype(jnp.bfloat16)

        def next_tile(i, carry, now=now, later=later, last=last):
            rows = rows_of(i)
            next_iter = quintic_one * now[rows, :].astype(jnp.float32) + jnp.dot(
                p_ref[rows, :], now[...], preferred_element_type=jnp.float32
            )
            if last:
                a_ref[rows, :] = (math.sqrt(extent) * next_iter).astype(jnp.bfloat16)
            else:
                later[rows, :] = next_iter.astype(jnp.bfloat16)
            return carry

        for i in range(tiles):
            next_tile(i, 0)

    chunks, quarter = out_ref.shape[0], out_ref.shape[1]
    span = TILE // quarter
    for i in range(chunks // span):
        reach = min(extent, (i + 1) * TILE)
        lanes = lax.broadcasted_iota(jnp.int32, (TILE, reach), 1)
        chosen = (place_ref[pl.ds(i * TILE, TILE), :] == lanes).astype(jnp.bfloat16)
        placed = jnp.dot(chosen, a_ref[:reach, :], preferred_element_type=jnp.float32)
        for q in range(quarter):
            out_ref[pl.ds(i * span, span), q, :] = placed[q * span : (q + 1) * span].astype(jnp.bfloat16)


def orthogonalize_kernel(slots, take, moment, place):
    extent = moment.shape[0]
    out_rows = (place.shape[0] // QUARTER, QUARTER, extent)
    square = (extent, extent)
    vmem = pl.BlockSpec(memory_space=pltpu.VMEM)
    return pl.pallas_call(
        newton_schulz_kernel,
        out_shape=(
            jax.ShapeDtypeStruct(out_rows, jnp.bfloat16),
            jax.ShapeDtypeStruct(square, jnp.float32),
        ),
        in_specs=[vmem, vmem, vmem, vmem],
        out_specs=(vmem, vmem),
        scratch_shapes=[pltpu.VMEM(square, jnp.bfloat16) for _ in range(5)],
        compiler_params=pltpu.CompilerParams(vmem_limit_bytes=48 * 1024 * 1024),
        cost_estimate=pl.CostEstimate(
            flops=2 * (3 * NS_ITERS + 2) * extent ** 3,
            bytes_accessed=16 * extent * extent,
            transcendentals=0,
        ),
    )(slots, take, moment, place)


def spare_pair(slots, take, moment, place):
    return (jnp.zeros((place.shape[0] // QUARTER, QUARTER, moment.shape[0]), jnp.bfloat16), jnp.zeros(moment.shape, jnp.float32))


def body(grad_rows, row_counts, owners, momentum):
    matrices, capacity, extent = grad_rows.shape
    shards = lax.axis_size("dp")
    dp_index = lax.axis_index("dp")
    rep_index = lax.axis_index("rep")
    slot_ids = slots_of(owners)
    matrix_ids = jnp.arange(matrices, dtype=jnp.int32)
    owner_ids = jnp.arange(shards, dtype=jnp.int32)
    in_lane = slot_ids == rep_index
    owned = owners[None, :] == owner_ids[:, None]
    earlier = (matrix_ids[:, None] < matrix_ids[None, :]).astype(jnp.float32)
    seen = jnp.dot(owned.astype(jnp.float32), earlier, precision=lax.Precision.HIGHEST)
    lane_pick = owned & (seen == rep_index.astype(jnp.float32))
    lane_matrix = jnp.sum(jnp.where(lane_pick, matrix_ids[None, :], 0), axis=1)
    send_table = jnp.take(grad_rows, lane_matrix, axis=0, mode="clip")
    arrived = lax.all_to_all(send_table, "dp", split_axis=0, concat_axis=0, tiled=True)

    held_here = (owners == dp_index) & in_lane
    active = jnp.any(held_here)
    counts = jnp.sum(jnp.where(held_here[:, None], row_counts, 0), axis=0)
    starts = exclusive_starts(counts)
    row_ids = jnp.arange(extent, dtype=jnp.int32)
    covers = (starts[None, :] <= row_ids[:, None]) & (row_ids[:, None] < (starts + counts)[None, :])
    holder = jnp.sum(jnp.where(covers, owner_ids[None, :], 0), axis=1)
    first_row = jnp.sum(jnp.where(covers, starts[None, :], 0), axis=1)
    row_index = holder * capacity + (row_ids - first_row)
    offsets = jnp.arange(capacity, dtype=jnp.int32)
    positions = starts[:, None] + offsets[None, :]
    usable = offsets[None, :] < counts[:, None]
    place = jnp.where(usable, positions, -1).reshape(-1, TILE // QUARTER, QUARTER)
    place = jnp.swapaxes(place, 1, 2).reshape(shards * capacity, 1)
    take, place, active = lax.optimization_barrier((row_index[:, None], place, active))
    outgoing, moment_new = lax.cond(
        active,
        orthogonalize_kernel,
        spare_pair,
        arrived.reshape(shards * capacity, extent),
        take,
        momentum[0, 0],
        place,
    )
    lanes = lax.axis_size("rep")
    quarter = capacity // lanes
    returned = lax.all_to_all(outgoing, ("dp", "rep"), split_axis=0, concat_axis=0, tiled=True)
    mine = jnp.take(returned.reshape(shards * lanes, quarter, extent), owners * lanes + slot_ids, axis=0, mode="clip")
    def shifted(block, step):
        return lax.ppermute(block, "rep", [(q, (q + step) % lanes) for q in range(lanes)])

    half = quarter // 2
    from_left = jnp.concatenate([shifted(mine[:, :half], 1), shifted(mine[:, half:], 1)], axis=1)
    from_right = jnp.concatenate(
        [shifted(mine[:, :half], lanes - 1), shifted(mine[:, half:], lanes - 1)], axis=1
    )
    from_far = jnp.concatenate(
        [shifted(mine[:, :half], 2), shifted(mine[:, half:], lanes - 2)], axis=1
    )
    picked_rows = jnp.zeros((matrices, capacity, extent), mine.dtype)
    for shift, block in ((0, mine), (1, from_left), (lanes - 1, from_right), (2, from_far)):
        source = (rep_index - shift + lanes) % lanes
        picked_rows = lax.dynamic_update_slice(picked_rows, block, (0, source * quarter, 0))
    return (picked_rows, moment_new[None, None])


def solution(mesh):
    return jax.shard_map(
        body,
        mesh=mesh,
        in_specs=(P(None, "dp", None), P(), P(), P("dp", "rep", None, None)),
        out_specs=(P(None, "dp", None), P("dp", "rep", None, None)),
        check_vma=False,
    )
```
